512 devices in a mesh: section: 8 (over x, core), ctx: 64 (over z, y).
Axes of the slice: x: 4, y: 8, z: 8, core: 2. Of those that a mesh axis runs over, the one named last changes fastest.
Arguments:
- inputs: bfloat16 [8, 1024, 8192], P('section', None, 'ctx'), may hold values from -6 to 6
- out_grad: bfloat16 [1024, 8192], P(None, 'ctx'), may hold values from -6 to 6
- filters: bfloat16 [8, 1024, 8192], P('section', 'ctx'), may hold values from -0.0625 to 0.0625
- conv_taps: float32 [8, 3, 7, 1024], P('section'), may hold values from -2.5 to 2.5
Outputs:
- in_grad: bfloat16 [8, 1024, 8192], P('section', None, 'ctx')
- filter_grad: float32 [8, 1024, 8192], P('section', 'ctx')
- tap_grad: float32 [8, 3, 7, 1024], P('section', None, None, 'ctx')
The draws below stay inside these ranges and needn't reach their ends.
All inputs are finite; a program needn't handle non-finite values.
Results may differ from the reference program's by a relative error of at most 0.014.
Values may be sent and summed in bfloat16 or wider, within the bound.
No kernel may reach another device: no remote copies, remote signals or barrier semaphores. Data moves between devices by JAX's collectives and lax.ppermute only.
A program may use at most 64 MiB of HBM per device.

```python
import jax
import jax.numpy as jnp

D = 1024
TAPS = 7
TOKENS = 8192
SECTIONS = 8


def steps_of(stream_key, extent, pieces, low, top_value):
    gain, own = 1.0, jax.random.fold_in(stream_key, 6)
    for position, parts in pieces:
        draws = jnp.exp(jax.random.uniform(jax.random.fold_in(own, position), (parts,), jnp.float32, low / len(pieces), top_value / len(pieces)))
        gain = gain * jnp.repeat(draws, extent[position] // parts).reshape([-1 if axis == position else 1 for axis in range(len(extent))])
    return gain


def noise(own_key, extent, deviation, bound, cuts=(), dtype=jnp.bfloat16):
    loudness = steps_of(own_key, extent, cuts, -0.22, 0.18) if cuts else 1.0
    array = jax.random.normal(own_key, extent, jnp.float32) * deviation * loudness
    return jnp.minimum(jnp.maximum(array, -bound), bound).astype(dtype)


def setup_inputs(seed: int = 0) -> dict:
    key_list = jax.random.split(jax.random.key(seed), 5)
    return {
        "inputs": noise(key_list[0], (SECTIONS, D, TOKENS), 1.0, 6.0, ((0, 8), (2, 64))),
        "out_grad": noise(key_list[1], (D, TOKENS), 1.0, 6.0, ((1, 64),)),
        "filters": noise(key_list[2], (SECTIONS, D, TOKENS), TOKENS ** -0.5, 0.0625, ((0, 8), (1, 64))),
        "conv_taps": noise(key_list[3], (SECTIONS, 3, TAPS, D), 0.34, 2.5, ((0, 8),), jnp.float32),
    }


def features(padded, weights, length):
    summed = jnp.zeros((3, padded.shape[0], length), jnp.float32)
    for offset in range(7):
        window = padded[:, 6 - offset:6 - offset + length].astype(jnp.float32)
        summed = summed + weights[:, offset, :, None] * window[None]
    return summed.astype(jnp.bfloat16)


def transposed(grad_all, weights):
    length = grad_all.shape[2]
    padded = jnp.pad(grad_all, ((0, 0), (0, 0), (0, 6)))
    summed = jnp.zeros(grad_all.shape[1:], jnp.float32)
    for offset in range(7):
        summed = summed + jnp.sum(weights[:, offset, :, None] * padded[:, :, offset:offset + length], axis=0)
    return summed


def tap_grads(padded, grad_all):
    length = grad_all.shape[2]
    per_offset = []
    for offset in range(7):
        window = padded[:, 6 - offset:6 - offset + length].astype(jnp.float32)
        per_offset.append(jnp.sum(grad_all * window[None], axis=2))
    return jnp.stack(per_offset, axis=1)


def reference(inputs, out_grad, filters, conv_taps):
    section_total = inputs.shape[0]
    length = inputs.shape[2]
    fft_len = 2 * length
    in_list = []
    filter_list = []
    tap_list = []
    carried = out_grad
    for section_idx in range(section_total - 1, -1, -1):
        weights = conv_taps[section_idx]
        padded = jnp.pad(inputs[section_idx], ((0, 0), (6, 0)))
        featured = features(padded, weights, length)
        query_feat = featured[0].astype(jnp.float32)
        key_feat = featured[1].astype(jnp.float32)
        value_feat = featured[2].astype(jnp.float32)
        mixed_kv = key_feat * value_feat
        spec_h = jnp.fft.rfft(filters[section_idx].astype(jnp.float32), n=fft_len, axis=1)
        spec_w = jnp.fft.rfft(mixed_kv, n=fft_len, axis=1)
        convolved = jnp.fft.irfft(spec_h * spec_w, n=fft_len, axis=1)[:, :length]
        grad_in = carried.astype(jnp.float32)
        grad_z = grad_in * query_feat
        grad_q = grad_in * convolved
        spec_dz = jnp.fft.rfft(grad_z, n=fft_len, axis=1)
        grad_w = jnp.fft.irfft(jnp.conj(spec_h) * spec_dz, n=fft_len, axis=1)[:, :length]
        grad_all = jnp.stack([grad_q, grad_w * value_feat, grad_w * key_feat])
        in_grad = transposed(grad_all, weights).astype(jnp.bfloat16)
        filter_grad = jnp.fft.irfft(jnp.conj(spec_w) * spec_dz, n=fft_len, axis=1)[:, :length]
        in_list.insert(0, in_grad)
        filter_list.insert(0, filter_grad)
        tap_list.insert(0, tap_grads(padded, grad_all))
        carried = in_grad
    return (jnp.stack(in_list), jnp.stack(filter_list), jnp.stack(tap_list))
```

```python
import math

import jax
import jax.numpy as jnp
from jax import lax
from jax.sharding import PartitionSpec as P

PRECISE = lax.Precision.HIGH


def shifted(block, axis, distance):
    devices = range(lax.axis_size(axis))
    route = [(i - distance, i) for i in devices if i - distance in devices]
    return lax.ppermute(block, axis, route)


def angle_table(row_count, col_count, modulus):
    row_ids = lax.broadcasted_iota(jnp.int32, (row_count, col_count), 0)
    col_ids = lax.broadcasted_iota(jnp.int32, (row_count, col_count), 1)
    product_mod = row_ids * col_ids % modulus
    angles = product_mod.astype(jnp.float32) * (2.0 * math.pi / modulus)
    return (jnp.cos(angles), jnp.sin(angles))


def make_tables(blocks_a, block_b):
    half_a = blocks_a // 2
    total_n = blocks_a * block_b
    return (
        angle_table(blocks_a, half_a, blocks_a),
        angle_table(half_a, blocks_a, blocks_a),
        angle_table(blocks_a, block_b, total_n),
        angle_table(block_b, block_b, block_b),
    )


def forward_spectrum(signal, tables):
    cos_one, sin_one = tables[0]
    cos_tw, sin_tw = tables[2]
    cos_two, sin_two = tables[3]
    channels = signal.shape[0]
    half_a = cos_one.shape[1]
    block_b = cos_two.shape[0]
    shaped = signal.reshape(channels, half_a, block_b)
    real_y = jnp.einsum("ka,cab->ckb", cos_one, shaped, precision=PRECISE)
    imag_y = -jnp.einsum("ka,cab->ckb", sin_one, shaped, precision=PRECISE)
    real_z = real_y * cos_tw + imag_y * sin_tw
    imag_z = imag_y * cos_tw - real_y * sin_tw
    real_x = jnp.einsum("ckb,mb->ckm", real_z, cos_two, precision=PRECISE) + jnp.einsum(
        "ckb,mb->ckm", imag_z, sin_two, precision=PRECISE
    )
    imag_x = jnp.einsum("ckb,mb->ckm", imag_z, cos_two, precision=PRECISE) - jnp.einsum(
        "ckb,mb->ckm", real_z, sin_two, precision=PRECISE
    )
    return (real_x, imag_x)


def inverse_signal(real_x, imag_x, tables):
    cos_one, sin_one = tables[1]
    cos_tw, sin_tw = tables[2]
    cos_two, sin_two = tables[3]
    channels = real_x.shape[0]
    half_a = cos_one.shape[0]
    block_b = cos_two.shape[0]
    total_n = cos_one.shape[1] * block_b
    real_p = jnp.einsum("ckm,mb->ckb", real_x, cos_two, precision=PRECISE) - jnp.einsum(
        "ckm,mb->ckb", imag_x, sin_two, precision=PRECISE
    )
    imag_p = jnp.einsum("ckm,mb->ckb", real_x, sin_two, precision=PRECISE) + jnp.einsum(
        "ckm,mb->ckb", imag_x, cos_two, precision=PRECISE
    )
    real_q = real_p * cos_tw - imag_p * sin_tw
    imag_q = real_p * sin_tw + imag_p * cos_tw
    summed = jnp.einsum("ak,ckb->cab", cos_one, real_q, precision=PRECISE) - jnp.einsum(
        "ak,ckb->cab", sin_one, imag_q, precision=PRECISE
    )
    return summed.reshape(channels, half_a * block_b) / total_n


def times_conj(real_a, imag_a, real_b, imag_b):
    return (real_a * real_b + imag_a * imag_b, real_a * imag_b - imag_a * real_b)


def features(padded, weights, length):
    summed = jnp.zeros((3, padded.shape[0], length), jnp.float32)
    for offset in range(7):
        window = padded[:, 6 - offset : 6 - offset + length].astype(jnp.float32)
        summed = summed + weights[:, offset, :, None] * window[None]
    return summed.astype(jnp.bfloat16)


def transposed(grad_all, weights):
    length = grad_all.shape[2]
    padded = jnp.pad(grad_all, ((0, 0), (0, 0), (0, 6)))
    summed = jnp.zeros(grad_all.shape[1:], jnp.float32)
    for offset in range(7):
        summed = summed + jnp.sum(
            weights[:, offset, :, None] * padded[:, :, offset : offset + length], axis=0
        )
    return summed


def tap_grads(padded, grad_all):
    length = grad_all.shape[2]
    per_offset = []
    for offset in range(7):
        window = padded[:, 6 - offset : 6 - offset + length].astype(jnp.float32)
        per_offset.append(jnp.sum(grad_all * window[None], axis=2))
    return jnp.stack(per_offset, axis=1)


def shards(inputs, out_grad, filters, conv_taps):
    sec_n = lax.axis_size("section")
    ctx_n = lax.axis_size("ctx")
    sec = lax.axis_index("section")
    ctx = lax.axis_index("ctx")
    channels = filters.shape[1]
    length = filters.shape[2]
    sub = channels // sec_n
    rows = sec_n * sub
    tok_dev = inputs.shape[2]
    x_ctx = lax.all_to_all(inputs, "ctx", split_axis=1, concat_axis=2, tiled=True)[0]
    x_all = lax.all_to_all(
        x_ctx.reshape(sec_n, sub, length), "section", split_axis=0, concat_axis=0, tiled=True
    )
    h_all = lax.all_to_all(
        filters[0].reshape(sec_n, sub, length), "section", split_axis=0, concat_axis=0, tiled=True
    )
    taps_c = lax.dynamic_slice_in_dim(conv_taps[0], ctx * channels, channels, 2)
    taps_c = jnp.moveaxis(taps_c.reshape(3, 7, sec_n, sub), 2, 0)
    taps_all = lax.all_to_all(taps_c, "section", split_axis=0, concat_axis=0, tiled=True)
    og = lax.dynamic_index_in_dim(
        out_grad.reshape(ctx_n, sec_n, sub, tok_dev), sec, 1, keepdims=False
    )
    og = lax.all_to_all(og, "ctx", split_axis=0, concat_axis=2, tiled=True)[0]
    x_pad = jnp.pad(x_all, ((0, 0), (0, 0), (6, 0)))
    summed = jnp.zeros((3, sec_n, sub, length), jnp.float32)
    for offset in range(7):
        window = x_pad[:, :, 6 - offset : 6 - offset + length].astype(jnp.float32)
        tap_w = jnp.moveaxis(taps_all[:, :, offset, :], 1, 0)
        summed = summed + tap_w[:, :, :, None] * window[None]
    featured = lax.reduce_precision(summed, exponent_bits=8, mantissa_bits=7)
    query_f, key_f, value_f = featured[0], featured[1], featured[2]
    tables = make_tables(2 * length // 128, 128)
    real_h, imag_h = forward_spectrum(h_all.reshape(rows, length).astype(jnp.float32), tables)
    real_w, imag_w = forward_spectrum((key_f * value_f).reshape(rows, length), tables)
    convolved = inverse_signal(
        real_h * real_w - imag_h * imag_w, real_h * imag_w + imag_h * real_w, tables
    ).reshape(sec_n, sub, length)
    carried = og.astype(jnp.float32)
    in_list = [None] * sec_n
    rd_list = [None] * sec_n
    id_list = [None] * sec_n
    grad_list = [None] * sec_n
    for layer in range(sec_n - 1, -1, -1):
        span = slice(layer * sub, (layer + 1) * sub)
        grad_in = carried
        grad_z = grad_in * query_f[layer]
        grad_q = grad_in * convolved[layer]
        real_d, imag_d = forward_spectrum(grad_z, tables)
        real_c, imag_c = times_conj(real_h[span], imag_h[span], real_d, imag_d)
        grad_w = inverse_signal(real_c, imag_c, tables)
        grad_all = jnp.stack([grad_q, grad_w * value_f[layer], grad_w * key_f[layer]])
        carried = lax.reduce_precision(
            transposed(grad_all, taps_all[layer]), exponent_bits=8, mantissa_bits=7
        )
        in_list[layer] = carried.astype(jnp.bfloat16)
        rd_list[layer] = real_d
        id_list[layer] = imag_d
        grad_list[layer] = grad_all
    real_d = jnp.concatenate(rd_list, axis=0)
    imag_d = jnp.concatenate(id_list, axis=0)
    real_c, imag_c = times_conj(real_w, imag_w, real_d, imag_d)
    filter_grad = inverse_signal(real_c, imag_c, tables).reshape(sec_n, sub, length)
    grads = jnp.stack(grad_list)
    taps_out = []
    for offset in range(7):
        window = x_pad[:, :, 6 - offset : 6 - offset + length].astype(jnp.float32)
        taps_out.append(jnp.sum(grads * window[:, None], axis=3))
    tap_grad = jnp.stack(taps_out, axis=2)
    in_all = jnp.stack(in_list)
    fg = lax.all_to_all(filter_grad, "section", split_axis=0, concat_axis=1, tiled=True)
    tg = lax.all_to_all(tap_grad, "section", split_axis=0, concat_axis=3, tiled=True)
    ig = lax.all_to_all(in_all, "section", split_axis=0, concat_axis=1, tiled=True)[0]
    ig = lax.all_to_all(ig, "ctx", split_axis=1, concat_axis=0, tiled=True)
    return (ig[None], fg, tg)


def solution(mesh):
    placed = (
        P("section", None, "ctx"),
        P(None, "ctx"),
        P("section", "ctx", None),
        P("section", None, None, None),
    )
    return jax.shard_map(
        shards,
        mesh=mesh,
        in_specs=placed,
        out_specs=(
            P("section", None, "ctx"),
            P("section", "ctx", None),
            P("section", None, None, "ctx"),
        ),
        check_vma=False,
    )
```

```python
import math

import jax
import jax.numpy as jnp
from jax import lax
from jax.experimental import pallas as pl
from jax.experimental.pallas import tpu as pltpu
from jax.sharding import PartitionSpec as P

LANES = 128


def angle_table(row_count, col_count, modulus):
    row_ids = lax.broadcasted_iota(jnp.int32, (row_count, col_count), 0)
    col_ids = lax.broadcasted_iota(jnp.int32, (row_count, col_count), 1)
    product_mod = row_ids * col_ids % modulus
    angles = product_mod.astype(jnp.float32) * (2.0 * math.pi / modulus)
    return (jnp.cos(angles), jnp.sin(angles))


def split_bf16(value):
    high = value.astype(jnp.bfloat16)
    low = (value - high.astype(jnp.float32)).astype(jnp.bfloat16)
    return high, low


def split_table(value):
    high = lax.reduce_precision(value, exponent_bits=8, mantissa_bits=7)
    return high.astype(jnp.bfloat16), (value - high).astype(jnp.bfloat16)


def mat(a, b):
    return jnp.dot(a, b, preferred_element_type=jnp.float32)


def dot_left(t_hi, t_lo, value):
    v_hi, v_lo = split_bf16(value)
    return mat(t_hi, v_hi) + mat(t_hi, v_lo) + mat(t_lo, v_hi)


def dot_right(value, t_hi, t_lo):
    v_hi, v_lo = split_bf16(value)
    return mat(v_hi, t_hi) + mat(v_lo, t_hi) + mat(v_hi, t_lo)


def spectrum_tables(length):
    half = length // LANES
    blocks = 2 * half
    total = blocks * LANES
    cos_one, sin_one = angle_table(blocks, half, blocks)
    cos_tw, sin_tw = angle_table(blocks, LANES, total)
    cos_two, sin_two = angle_table(LANES, LANES, LANES)
    first = jnp.concatenate([cos_one, -sin_one], axis=0)
    forward = jnp.concatenate(
        [jnp.concatenate([cos_two, -sin_two], 1), jnp.concatenate([sin_two, cos_two], 1)], 0
    )
    backward = jnp.concatenate(
        [jnp.concatenate([cos_two, sin_two], 1), jnp.concatenate([-sin_two, cos_two], 1)], 0
    )
    last = jnp.concatenate([cos_one.T, -sin_one.T], axis=1) / total
    return (
        *split_table(first),
        cos_tw,
        sin_tw,
        *split_table(forward),
        *split_table(backward),
        *split_table(last),
    )


def chain_kernel(
    sub, taps_ref, x_ref, h_ref, og_ref, a1h, a1l, tcr, tsr, w2h, w2l, wbh, wbl, a3h, a3l,
    in_ref, fg_ref, tp_ref, q_s, k_s, v_s, conv_s, hs_s, ws_s, ds_s,
):
    layers, rows, lanes = x_ref.shape
    half = rows // sub
    blocks = 2 * half
    row_id = lax.broadcasted_iota(jnp.int32, (rows, lanes), 0)
    lane_id = lax.broadcasted_iota(jnp.int32, (rows, lanes), 1)
    first_row = row_id == 0
    last_row = row_id == half - 1
    for c in range(1, sub):
        first_row = first_row | (row_id == c * half)
        last_row = last_row | (row_id == c * half + half - 1)

    def fft(signal):
        twc = tcr[...]
        tws = tsr[...]
        parts = []
        for c in range(sub):
            y = dot_left(a1h[...], a1l[...], signal[c * half:(c + 1) * half, :])
            yr, yi = y[:blocks], y[blocks:]
            parts.append(jnp.concatenate([yr * twc + yi * tws, yi * twc - yr * tws], axis=1))
        return dot_right(jnp.concatenate(parts, axis=0), w2h[...], w2l[...])

    def ifft(spec):
        twc = tcr[...]
        tws = tsr[...]
        p = dot_right(spec, wbh[...], wbl[...])
        outs = []
        for c in range(sub):
            pr = p[c * blocks:(c + 1) * blocks, :lanes]
            pi = p[c * blocks:(c + 1) * blocks, lanes:]
            q = jnp.concatenate([pr * twc - pi * tws, pr * tws + pi * twc], axis=0)
            outs.append(dot_left(a3h[...], a3l[...], q))
        return jnp.concatenate(outs, axis=0)

    def back(value, j):
        if j == 0:
            return value
        r1 = pltpu.roll(value, j, 1)
        r2 = pltpu.roll(r1, 1, 0)
        out = jnp.where(lane_id >= j, r1, r2)
        return jnp.where(first_row & (lane_id < j), 0.0, out)

    def ahead(value, j):
        if j == 0:
            return value
        r1 = pltpu.roll(value, lanes - j, 1)
        r2 = pltpu.roll(r1, rows - 1, 0)
        out = jnp.where(lane_id < lanes - j, r1, r2)
        return jnp.where(last_row & (lane_id >= lanes - j), 0.0, out)

    def tap(layer, i, j):
        base = ((layer * 3 + i) * 7 + j) * sub
        w = jnp.full((rows, lanes), taps_ref[base + sub - 1], jnp.float32)
        for c in range(sub - 2, -1, -1):
            w = jnp.where(row_id < (c + 1) * half, taps_ref[base + c], w)
        return w

    def real_imag(spec):
        return spec[:, :lanes], spec[:, lanes:]

    def phase_one(layer, carry):
        x = x_ref[layer].astype(jnp.float32)
        feats = [jnp.zeros((rows, lanes), jnp.float32) for _ in range(3)]
        for j in range(7):
            xs = back(x, j)
            for i in range(3):
                feats[i] = feats[i] + tap(layer, i, j) * xs
        q, k, v = [f.astype(jnp.bfloat16).astype(jnp.float32) for f in feats]
        q_s[layer] = q
        k_s[layer] = k
        v_s[layer] = v
        hspec = fft(h_ref[layer].astype(jnp.float32))
        wspec = fft(k * v)
        hs_s[layer] = hspec
        ws_s[layer] = wspec
        hr, hi = real_imag(hspec)
        wr, wi = real_imag(wspec)
        conv_s[layer] = ifft(jnp.concatenate([hr * wr - hi * wi, hr * wi + hi * wr], axis=1))
        return carry

    lax.fori_loop(0, layers, phase_one, 0)

    def phase_two(step, carried):
        layer = layers - 1 - step
        grad_z = carried * q_s[layer]
        grad_q = carried * conv_s[layer]
        dspec = fft(grad_z)
        ds_s[layer] = dspec
        hr, hi = real_imag(hs_s[layer])
        dr, di = real_imag(dspec)
        grad_w = ifft(jnp.concatenate([hr * dr + hi * di, hr * di - hi * dr], axis=1))
        grads = (grad_q, grad_w * v_s[layer], grad_w * k_s[layer])
        summed = jnp.zeros((rows, lanes), jnp.float32)
        for j in range(7):
            term = tap(layer, 0, j) * ahead(grads[0], j)
            term = term + tap(layer, 1, j) * ahead(grads[1], j)
            term = term + tap(layer, 2, j) * ahead(grads[2], j)
            summed = summed + term
        rounded = summed.astype(jnp.bfloat16)
        in_ref[layer] = rounded
        x = x_ref[layer].astype(jnp.float32)
        for j in range(7):
            xs = back(x, j)
            for i in range(3):
                prod = grads[i] * xs
                for c in range(sub):
                    row = (i * 7 + j) * sub + c
                    part = jnp.sum(prod[c * half:(c + 1) * half, :], axis=0, keepdims=True)
                    tp_ref[layer, pl.ds(row, 1), :] = part
        return rounded.astype(jnp.float32)

    lax.fori_loop(0, layers, phase_two, og_ref[...].astype(jnp.float32))

    def phase_three(layer, carry):
        wr, wi = real_imag(ws_s[layer])
        dr, di = real_imag(ds_s[layer])
        fg_ref[layer] = ifft(jnp.concatenate([wr * dr + wi * di, wr * di - wi * dr], axis=1))
        return carry

    lax.fori_loop(0, layers, phase_three, 0)


def run_chain(x_all, h_all, og, taps_all):
    layers, sub, length = x_all.shape
    half = length // LANES
    rows = sub * half
    blocks = 2 * half
    tables = spectrum_tables(length)
    vmem = pl.BlockSpec(memory_space=pltpu.VMEM)
    spec_shape = pltpu.VMEM((layers, sub * blocks, 2 * LANES), jnp.float32)
    sig_shape = pltpu.VMEM((layers, rows, LANES), jnp.float32)
    in_k, fg_k, tp_k = pl.pallas_call(
        lambda *refs: chain_kernel(sub, *refs),
        out_shape=(
            jax.ShapeDtypeStruct((layers, rows, LANES), jnp.bfloat16),
            jax.ShapeDtypeStruct((layers, rows, LANES), jnp.float32),
            jax.ShapeDtypeStruct((layers, 21 * sub, LANES), jnp.float32),
        ),
        in_specs=[pl.BlockSpec(memory_space=pltpu.SMEM)] + [vmem] * 13,
        out_specs=(vmem, vmem, vmem),
        scratch_shapes=[sig_shape] * 4 + [spec_shape] * 3,
        compiler_params=pltpu.CompilerParams(vmem_limit_bytes=48 * 1024 * 1024),
        name="hyena_chain",
    )(
        taps_all.reshape(-1),
        x_all.reshape(layers, rows, LANES),
        h_all.reshape(layers, rows, LANES),
        og.reshape(rows, LANES),
        *tables,
    )
    tap_grad = jnp.sum(tp_k, axis=2).reshape(layers, 3, 7, sub)
    return in_k.reshape(layers, sub, length), fg_k.reshape(layers, sub, length), tap_grad


def shards(inputs, out_grad, filters, conv_taps):
    sec_n = lax.axis_size("section")
    ctx_n = lax.axis_size("ctx")
    sec = lax.axis_index("section")
    ctx = lax.axis_index("ctx")
    channels = filters.shape[1]
    length = filters.shape[2]
    sub = channels // sec_n
    tok_dev = inputs.shape[2]
    x_ctx = lax.all_to_all(inputs, "ctx", split_axis=1, concat_axis=2, tiled=True)[0]
    x_all = lax.all_to_all(
        x_ctx.reshape(sec_n, sub, length), "section", split_axis=0, concat_axis=0, tiled=True
    )
    h_all = lax.all_to_all(
        filters[0].reshape(sec_n, sub, length), "section", split_axis=0, concat_axis=0, tiled=True
    )
    taps_c = lax.dynamic_slice_in_dim(conv_taps[0], ctx * channels, channels, 2)
    taps_c = jnp.moveaxis(taps_c.reshape(3, 7, sec_n, sub), 2, 0)
    taps_all = lax.all_to_all(taps_c, "section", split_axis=0, concat_axis=0, tiled=True)
    og = lax.dynamic_index_in_dim(
        out_grad.reshape(ctx_n, sec_n, sub, tok_dev), sec, 1, keepdims=False
    )
    og = lax.all_to_all(og, "ctx", split_axis=0, concat_axis=2, tiled=True)[0]
    in_all, filter_grad, tap_grad = run_chain(x_all, h_all, og, taps_all)
    fg = lax.all_to_all(filter_grad, "section", split_axis=0, concat_axis=1, tiled=True)
    tg = lax.all_to_all(tap_grad, "section", split_axis=0, concat_axis=3, tiled=True)
    ig = lax.all_to_all(in_all, "section", split_axis=0, concat_axis=1, tiled=True)[0]
    ig = lax.all_to_all(ig, "ctx", split_axis=1, concat_axis=0, tiled=True)
    return (ig[None], fg, tg)


def solution(mesh):
    placed = (
        P("section", None, "ctx"),
        P(None, "ctx"),
        P("section", "ctx", None),
        P("section", None, None, None),
    )
    return jax.shard_map(
        shards,
        mesh=mesh,
        in_specs=placed,
        out_specs=(
            P("section", None, "ctx"),
            P("section", "ctx", None),
            P("section", None, None, "ctx"),
        ),
        check_vma=False,
    )
```

```python
import math

import jax
import jax.numpy as jnp
from jax import lax
from jax.experimental import pallas as pl
from jax.experimental.pallas import tpu as pltpu
from jax.sharding import PartitionSpec as P

LANES = 128


def angle_table(row_count, col_count, modulus):
    row_ids = lax.broadcasted_iota(jnp.int32, (row_count, col_count), 0)
    col_ids = lax.broadcasted_iota(jnp.int32, (row_count, col_count), 1)
    product_mod = row_ids * col_ids % modulus
    angles = product_mod.astype(jnp.float32) * (2.0 * math.pi / modulus)
    return (jnp.cos(angles), jnp.sin(angles))


def split_bf16(value):
    high = value.astype(jnp.bfloat16)
    low = (value - high.astype(jnp.float32)).astype(jnp.bfloat16)
    return high, low


def split_table(value):
    high = lax.reduce_precision(value, exponent_bits=8, mantissa_bits=7)
    return high.astype(jnp.bfloat16), (value - high).astype(jnp.bfloat16)


def mat(a, b):
    return jnp.dot(a, b, preferred_element_type=jnp.float32)


def dot_left(t_hi, t_lo, value):
    v_hi, v_lo = split_bf16(value)
    return mat(t_hi, v_hi) + mat(t_hi, v_lo) + mat(t_lo, v_hi)


def dot_right(value, t_hi, t_lo):
    v_hi, v_lo = split_bf16(value)
    return mat(v_hi, t_hi) + mat(v_lo, t_hi) + mat(v_hi, t_lo)


def spectrum_tables(length):
    half = length // LANES
    blocks = 2 * half
    total = blocks * LANES
    cos_one, sin_one = angle_table(blocks, half, blocks)
    cos_tw, sin_tw = angle_table(blocks, LANES, total)
    cos_two, sin_two = angle_table(LANES, LANES, LANES)
    first = jnp.concatenate([cos_one, -sin_one], axis=0)
    forward = jnp.concatenate(
        [jnp.concatenate([cos_two, -sin_two], 1), jnp.concatenate([sin_two, cos_two], 1)], 0
    )
    backward = jnp.concatenate(
        [jnp.concatenate([cos_two, sin_two], 1), jnp.concatenate([-sin_two, cos_two], 1)], 0
    )
    last = jnp.concatenate([cos_one.T, -sin_one.T], axis=1) / total
    return (
        *split_table(first),
        cos_tw,
        sin_tw,
        *split_table(forward),
        *split_table(backward),
        *split_table(last),
    )


def chain_kernel(
    sub, taps_ref, x_ref, h_ref, og_ref, a1h, a1l, tcr, tsr, w2h, w2l, wbh, wbl, a3h, a3l,
    in_ref, fg_ref, tp_ref, q_s, k_s, v_s, conv_s, hs_s, ws_s, ds_s,
):
    layers, rows, lanes = x_ref.shape
    half = rows // sub
    blocks = 2 * half
    row_id = lax.broadcasted_iota(jnp.int32, (rows, lanes), 0)
    lane_id = lax.broadcasted_iota(jnp.int32, (rows, lanes), 1)
    first_row = row_id == 0
    last_row = row_id == half - 1
    for c in range(1, sub):
        first_row = first_row | (row_id == c * half)
        last_row = last_row | (row_id == c * half + half - 1)

    def fft(signal):
        twc = tcr[...]
        tws = tsr[...]
        parts = []
        for c in range(sub):
            y = dot_left(a1h[...], a1l[...], signal[c * half:(c + 1) * half, :])
            yr, yi = y[:blocks], y[blocks:]
            parts.append(jnp.concatenate([yr * twc + yi * tws, yi * twc - yr * tws], axis=1))
        return dot_right(jnp.concatenate(parts, axis=0), w2h[...], w2l[...])

    def ifft(spec):
        twc = tcr[...]
        tws = tsr[...]
        p = dot_right(spec, wbh[...], wbl[...])
        outs = []
        for c in range(sub):
            pr = p[c * blocks:(c + 1) * blocks, :lanes]
            pi = p[c * blocks:(c + 1) * blocks, lanes:]
            q = jnp.concatenate([pr * twc - pi * tws, pr * tws + pi * twc], axis=0)
            outs.append(dot_left(a3h[...], a3l[...], q))
        return jnp.concatenate(outs, axis=0)

    def back(value, j):
        if j == 0:
            return value
        r1 = pltpu.roll(value, j, 1)
        r2 = pltpu.roll(r1, 1, 0)
        out = jnp.where(lane_id >= j, r1, r2)
        return jnp.where(first_row & (lane_id < j), 0.0, out)

    def ahead(value, j):
        if j == 0:
            return value
        r1 = pltpu.roll(value, lanes - j, 1)
        r2 = pltpu.roll(r1, rows - 1, 0)
        out = jnp.where(lane_id < lanes - j, r1, r2)
        return jnp.where(last_row & (lane_id >= lanes - j), 0.0, out)

    def tap(layer, i, j):
        base = ((layer * 3 + i) * 7 + j) * sub
        w = jnp.full((rows, lanes), taps_ref[base + sub - 1], jnp.float32)
        for c in range(sub - 2, -1, -1):
            w = jnp.where(row_id < (c + 1) * half, taps_ref[base + c], w)
        return w

    def real_imag(spec):
        return spec[:, :lanes], spec[:, lanes:]

    def phase_one(layer, carry):
        x = x_ref[layer].astype(jnp.float32)
        feats = [jnp.zeros((rows, lanes), jnp.float32) for _ in range(3)]
        for j in range(7):
            xs = back(x, j)
            for i in range(3):
                feats[i] = feats[i] + tap(layer, i, j) * xs
        q, k, v = [f.astype(jnp.bfloat16).astype(jnp.float32) for f in feats]
        q_s[layer] = q
        k_s[layer] = k
        v_s[layer] = v
        hspec = fft(h_ref[layer].astype(jnp.float32))
        wspec = fft(k * v)
        hs_s[layer] = hspec
        ws_s[layer] = wspec
        hr, hi = real_imag(hspec)
        wr, wi = real_imag(wspec)
        conv_s[layer] = ifft(jnp.concatenate([hr * wr - hi * wi, hr * wi + hi * wr], axis=1))
        return carry

    lax.fori_loop(0, layers, phase_one, 0)

    def phase_two(step, carried):
        layer = layers - 1 - step
        grad_z = carried * q_s[layer]
        grad_q = carried * conv_s[layer]
        dspec = fft(grad_z)
        ds_s[layer] = dspec
        hr, hi = real_imag(hs_s[layer])
        dr, di = real_imag(dspec)
        grad_w = ifft(jnp.concatenate([hr * dr + hi * di, hr * di - hi * dr], axis=1))
        grads = (grad_q, grad_w * v_s[layer], grad_w * k_s[layer])
        summed = jnp.zeros((rows, lanes), jnp.float32)
        for j in range(7):
            term = tap(layer, 0, j) * ahead(grads[0], j)
            term = term + tap(layer, 1, j) * ahead(grads[1], j)
            term = term + tap(layer, 2, j) * ahead(grads[2], j)
            summed = summed + term
        rounded = summed.astype(jnp.bfloat16)
        in_ref[layer] = rounded
        x = x_ref[layer].astype(jnp.float32)
        for j in range(7):
            xs = back(x, j)
            for i in range(3):
                prod = grads[i] * xs
                for c in range(sub):
                    row = (i * 7 + j) * sub + c
                    part = jnp.sum(prod[c * half:(c + 1) * half, :], axis=0, keepdims=True)
                    tp_ref[layer, pl.ds(row, 1), :] = part
        return rounded.astype(jnp.float32)

    lax.fori_loop(0, layers, phase_two, og_ref[...].astype(jnp.float32))

    def phase_three(layer, carry):
        wr, wi = real_imag(ws_s[layer])
        dr, di = real_imag(ds_s[layer])
        fg_ref[layer] = ifft(jnp.concatenate([wr * dr + wi * di, wr * di - wi * dr], axis=1))
        return carry

    lax.fori_loop(0, layers, phase_three, 0)


def run_chain(x_all, h_all, og, taps_all):
    layers, sub, length = x_all.shape
    half = length // LANES
    rows = sub * half
    blocks = 2 * half
    tables = spectrum_tables(length)
    vmem = pl.BlockSpec(memory_space=pltpu.VMEM)
    spec_shape = pltpu.VMEM((layers, sub * blocks, 2 * LANES), jnp.float32)
    sig_shape = pltpu.VMEM((layers, rows, LANES), jnp.float32)
    in_k, fg_k, tp_k = pl.pallas_call(
        lambda *refs: chain_kernel(sub, *refs),
        out_shape=(
            jax.ShapeDtypeStruct((layers, rows, LANES), jnp.bfloat16),
            jax.ShapeDtypeStruct((layers, rows, LANES), jnp.float32),
            jax.ShapeDtypeStruct((layers, 21 * sub, LANES), jnp.float32),
        ),
        in_specs=[pl.BlockSpec(memory_space=pltpu.SMEM)] + [vmem] * 13,
        out_specs=(vmem, vmem, vmem),
        scratch_shapes=[sig_shape] * 4 + [spec_shape] * 3,
        compiler_params=pltpu.CompilerParams(vmem_limit_bytes=48 * 1024 * 1024),
        name="hyena_chain",
    )(
        taps_all.reshape(-1),
        x_all.reshape(layers, rows, LANES),
        h_all.reshape(layers, rows, LANES),
        og.reshape(rows, LANES),
        *tables,
    )
    tap_grad = jnp.sum(tp_k, axis=2).reshape(layers, 3, 7, sub)
    return in_k.reshape(layers, sub, length), fg_k.reshape(layers, sub, length), tap_grad


def exact_pieces(value):
    pieces = []
    rest = value
    for _ in range(3):
        high = lax.reduce_precision(rest, exponent_bits=8, mantissa_bits=7)
        pieces.append(high.astype(jnp.bfloat16))
        rest = rest - high
    return jnp.concatenate(pieces, axis=-1)


def joined(pieces):
    third = pieces.shape[-1] // 3
    parts = [pieces[..., i * third:(i + 1) * third].astype(jnp.float32) for i in range(3)]
    return parts[0] + parts[1] + parts[2]


def shards(inputs, out_grad, filters, conv_taps):
    sec_n = lax.axis_size("section")
    ctx_n = lax.axis_size("ctx")
    sec = lax.axis_index("section")
    ctx = lax.axis_index("ctx")
    channels = filters.shape[1]
    length = filters.shape[2]
    sub = channels // sec_n
    tok_dev = inputs.shape[2]
    span = sub * length
    og = lax.dynamic_index_in_dim(
        out_grad.reshape(ctx_n, sec_n, sub, tok_dev), sec, 1, keepdims=False
    )
    sent = jnp.concatenate([inputs[0].reshape(ctx_n, channels, tok_dev), og], axis=1)
    got = lax.all_to_all(sent, "ctx", split_axis=0, concat_axis=2, tiled=True)[0]
    x_ctx = got[:channels]
    og = got[channels:]
    taps_c = lax.dynamic_slice_in_dim(conv_taps[0], ctx * channels, channels, 2)
    taps_c = jnp.moveaxis(taps_c.reshape(3, 7, sec_n, sub), 2, 0).reshape(sec_n, 21 * sub)
    sent = jnp.concatenate(
        [
            x_ctx.reshape(sec_n, span),
            filters[0].reshape(sec_n, span),
            exact_pieces(taps_c),
        ],
        axis=1,
    )
    got = lax.all_to_all(sent, "section", split_axis=0, concat_axis=0, tiled=True)
    x_all = got[:, :span].reshape(sec_n, sub, length)
    h_all = got[:, span:2 * span].reshape(sec_n, sub, length)
    taps_all = joined(got[:, 2 * span:]).reshape(sec_n, 3, 7, sub)
    in_all, filter_grad, tap_grad = run_chain(x_all, h_all, og, taps_all)
    sent = jnp.concatenate(
        [
            filter_grad.reshape(sec_n, span),
            in_all.reshape(sec_n, span).astype(jnp.float32),
            tap_grad.reshape(sec_n, 21 * sub),
        ],
        axis=1,
    )
    got = lax.all_to_all(sent, "section", split_axis=0, concat_axis=0, tiled=True)
    fg = got[:, :span].reshape(1, channels, length)
    ig = got[:, span:2 * span].astype(jnp.bfloat16).reshape(channels, length)
    tg = jnp.moveaxis(got[:, 2 * span:].reshape(sec_n, 3, 7, sub), 0, 2)
    tg = tg.reshape(1, 3, 7, channels)
    ig = lax.all_to_all(ig, "ctx", split_axis=1, concat_axis=0, tiled=True)
    return (ig[None], fg, tg)


def solution(mesh):
    placed = (
        P("section", None, "ctx"),
        P(None, "ctx"),
        P("section", "ctx", None),
        P("section", None, None, None),
    )
    return jax.shard_map(
        shards,
        mesh=mesh,
        in_specs=placed,
        out_specs=(
            P("section", None, "ctx"),
            P("section", "ctx", None),
            P("section", None, None, "ctx"),
        ),
        check_vma=False,
    )
```

```python
import math

import jax
import jax.numpy as jnp
from jax import lax
from jax.experimental import pallas as pl
from jax.experimental.pallas import tpu as pltpu
from jax.sharding import PartitionSpec as P

LANES = 128


def angle_table(row_count, col_count, modulus):
    row_ids = lax.broadcasted_iota(jnp.int32, (row_count, col_count), 0)
    col_ids = lax.broadcasted_iota(jnp.int32, (row_count, col_count), 1)
    product_mod = row_ids * col_ids % modulus
    angles = product_mod.astype(jnp.float32) * (2.0 * math.pi / modulus)
    return (jnp.cos(angles), jnp.sin(angles))


def split_bf16(value):
    high = value.astype(jnp.bfloat16)
    low = (value - high.astype(jnp.float32)).astype(jnp.bfloat16)
    return high, low


def split_table(value):
    high = lax.reduce_precision(value, exponent_bits=8, mantissa_bits=7)
    return high.astype(jnp.bfloat16), (value - high).astype(jnp.bfloat16)


def mat(a, b):
    return jnp.dot(a, b, preferred_element_type=jnp.float32)


def dot_left(t_hi, t_lo, value):
    v_hi, v_lo = split_bf16(value)
    return mat(t_hi, v_hi) + mat(t_hi, v_lo) + mat(t_lo, v_hi)


def dot_right(value, t_hi, t_lo):
    v_hi, v_lo = split_bf16(value)
    return mat(v_hi, t_hi) + mat(v_lo, t_hi) + mat(v_hi, t_lo)


def spectrum_tables(length):
    half = length // LANES
    blocks = 2 * half
    total = blocks * LANES
    cos_one, sin_one = angle_table(blocks, half, blocks)
    cos_tw, sin_tw = angle_table(blocks, LANES, total)
    cos_two, sin_two = angle_table(LANES, LANES, LANES)
    first = jnp.concatenate([cos_one, -sin_one], axis=0)
    forward = jnp.concatenate(
        [jnp.concatenate([cos_two, -sin_two], 1), jnp.concatenate([sin_two, cos_two], 1)], 0
    )
    backward = jnp.concatenate(
        [jnp.concatenate([cos_two, sin_two], 1), jnp.concatenate([-sin_two, cos_two], 1)], 0
    )
    last = jnp.concatenate([cos_one.T, -sin_one.T], axis=1) / total
    return (
        *split_table(first),
        cos_tw,
        sin_tw,
        *split_table(forward),
        *split_table(backward),
        *split_table(last),
    )


def chain_kernel(
    sub, taps_ref, x_ref, h_ref, og_ref, a1h, a1l, tcr, tsr, w2h, w2l, wbh, wbl, a3h, a3l,
    in_ref, fg_ref, tp_ref, q_s, k_s, v_s, conv_s, hs_s, ws_s, ds_s,
):
    layers, rows, lanes = x_ref.shape
    half = rows // sub
    blocks = 2 * half
    row_id = lax.broadcasted_iota(jnp.int32, (rows, lanes), 0)
    lane_id = lax.broadcasted_iota(jnp.int32, (rows, lanes), 1)
    first_row = row_id == 0
    last_row = row_id == half - 1
    for c in range(1, sub):
        first_row = first_row | (row_id == c * half)
        last_row = last_row | (row_id == c * half + half - 1)

    def fft(signal):
        twc = tcr[...]
        tws = tsr[...]
        parts = []
        for c in range(sub):
            y = dot_left(a1h[...], a1l[...], signal[c * half:(c + 1) * half, :])
            yr, yi = y[:blocks], y[blocks:]
            parts.append(jnp.concatenate([yr * twc + yi * tws, yi * twc - yr * tws], axis=1))
        return dot_right(jnp.concatenate(parts, axis=0), w2h[...], w2l[...])

    def ifft(spec):
        twc = tcr[...]
        tws = tsr[...]
        p = dot_right(spec, wbh[...], wbl[...])
        outs = []
        for c in range(sub):
            pr = p[c * blocks:(c + 1) * blocks, :lanes]
            pi = p[c * blocks:(c + 1) * blocks, lanes:]
            q = jnp.concatenate([pr * twc - pi * tws, pr * tws + pi * twc], axis=0)
            outs.append(dot_left(a3h[...], a3l[...], q))
        return jnp.concatenate(outs, axis=0)

    def back(value, j):
        if j == 0:
            return value
        r1 = pltpu.roll(value, j, 1)
        r2 = pltpu.roll(r1, 1, 0)
        out = jnp.where(lane_id >= j, r1, r2)
        return jnp.where(first_row & (lane_id < j), 0.0, out)

    def ahead(value, j):
        if j == 0:
            return value
        r1 = pltpu.roll(value, lanes - j, 1)
        r2 = pltpu.roll(r1, rows - 1, 0)
        out = jnp.where(lane_id < lanes - j, r1, r2)
        return jnp.where(last_row & (lane_id >= lanes - j), 0.0, out)

    def tap(layer, i, j):
        base = ((layer * 3 + i) * 7 + j) * sub
        w = jnp.full((rows, lanes), taps_ref[base + sub - 1], jnp.float32)
        for c in range(sub - 2, -1, -1):
            w = jnp.where(row_id < (c + 1) * half, taps_ref[base + c], w)
        return w

    def real_imag(spec):
        return spec[:, :lanes], spec[:, lanes:]

    def phase_one(layer, carry):
        x = x_ref[layer].astype(jnp.float32)
        feats = [jnp.zeros((rows, lanes), jnp.float32) for _ in range(3)]
        for j in range(7):
            xs = back(x, j)
            for i in range(3):
                feats[i] = feats[i] + tap(layer, i, j) * xs
        q, k, v = [f.astype(jnp.bfloat16).astype(jnp.float32) for f in feats]
        q_s[layer] = q
        k_s[layer] = k
        v_s[layer] = v
        hspec = fft(h_ref[layer].astype(jnp.float32))
        wspec = fft(k * v)
        hs_s[layer] = hspec
        ws_s[layer] = wspec
        hr, hi = real_imag(hspec)
        wr, wi = real_imag(wspec)
        conv_s[layer] = ifft(jnp.concatenate([hr * wr - hi * wi, hr * wi + hi * wr], axis=1))
        return carry

    lax.fori_loop(0, layers, phase_one, 0)

    def phase_two(step, carried):
        layer = layers - 1 - step
        grad_z = carried * q_s[layer]
        grad_q = carried * conv_s[layer]
        dspec = fft(grad_z)
        ds_s[layer] = dspec
        hr, hi = real_imag(hs_s[layer])
        dr, di = real_imag(dspec)
        grad_w = ifft(jnp.concatenate([hr * dr + hi * di, hr * di - hi * dr], axis=1))
        grads = (grad_q, grad_w * v_s[layer], grad_w * k_s[layer])
        summed = jnp.zeros((rows, lanes), jnp.float32)
        for j in range(7):
            term = tap(layer, 0, j) * ahead(grads[0], j)
            term = term + tap(layer, 1, j) * ahead(grads[1], j)
            term = term + tap(layer, 2, j) * ahead(grads[2], j)
            summed = summed + term
        rounded = summed.astype(jnp.bfloat16)
        in_ref[layer] = rounded
        x = x_ref[layer].astype(jnp.float32)
        for j in range(7):
            xs = back(x, j)
            for i in range(3):
                prod = grads[i] * xs
                for c in range(sub):
                    row = (i * 7 + j) * sub + c
                    part = jnp.sum(prod[c * half:(c + 1) * half, :], axis=0, keepdims=True)
                    tp_ref[layer, pl.ds(row, 1), :] = part
        return rounded.astype(jnp.float32)

    lax.fori_loop(0, layers, phase_two, og_ref[...].astype(jnp.float32))

    def phase_three(layer, carry):
        wr, wi = real_imag(ws_s[layer])
        dr, di = real_imag(ds_s[layer])
        fg_ref[layer] = ifft(jnp.concatenate([wr * dr + wi * di, wr * di - wi * dr], axis=1))
        return carry

    lax.fori_loop(0, layers, phase_three, 0)


def run_chain(x_all, h_all, og, taps_all):
    layers, rows, _ = x_all.shape
    sub = taps_all.shape[3]
    half = rows // sub
    length = half * LANES
    blocks = 2 * half
    tables = spectrum_tables(length)
    vmem = pl.BlockSpec(memory_space=pltpu.VMEM)
    spec_shape = pltpu.VMEM((layers, sub * blocks, 2 * LANES), jnp.float32)
    sig_shape = pltpu.VMEM((layers, rows, LANES), jnp.float32)
    in_k, fg_k, tp_k = pl.pallas_call(
        lambda *refs: chain_kernel(sub, *refs),
        out_shape=(
            jax.ShapeDtypeStruct((layers, rows, LANES), jnp.bfloat16),
            jax.ShapeDtypeStruct((layers, rows, LANES), jnp.float32),
            jax.ShapeDtypeStruct((layers, 21 * sub, LANES), jnp.float32),
        ),
        in_specs=[pl.BlockSpec(memory_space=pltpu.SMEM)] + [vmem] * 13,
        out_specs=(vmem, vmem, vmem),
        scratch_shapes=[sig_shape] * 4 + [spec_shape] * 3,
        compiler_params=pltpu.CompilerParams(vmem_limit_bytes=48 * 1024 * 1024),
        name="hyena_chain",
    )(
        taps_all.reshape(-1),
        x_all,
        h_all,
        og.reshape(rows, LANES),
        *tables,
    )
    tap_grad = jnp.sum(tp_k, axis=2).reshape(layers, 3, 7, sub)
    return in_k.reshape(layers, sub, length), fg_k.reshape(layers, sub, length), tap_grad


def exact_pieces(value):
    pieces = []
    rest = value
    for _ in range(3):
        high = lax.reduce_precision(rest, exponent_bits=8, mantissa_bits=7)
        pieces.append(high.astype(jnp.bfloat16))
        rest = rest - high
    return jnp.concatenate(pieces, axis=-1)


def joined(pieces):
    third = pieces.shape[-1] // 3
    parts = [pieces[..., i * third:(i + 1) * third].astype(jnp.float32) for i in range(3)]
    return parts[0] + parts[1] + parts[2]


def shards(inputs, out_grad, filters, conv_taps):
    sec_n = lax.axis_size("section")
    ctx_n = lax.axis_size("ctx")
    sec = lax.axis_index("section")
    ctx = lax.axis_index("ctx")
    channels = filters.shape[1]
    length = filters.shape[2]
    sub = channels // sec_n
    tok_dev = inputs.shape[2]
    span = sub * length
    og = lax.dynamic_index_in_dim(
        out_grad.reshape(ctx_n, sec_n, sub, tok_dev), sec, 1, keepdims=False
    )
    sent = jnp.concatenate([inputs[0].reshape(ctx_n, channels, tok_dev), og], axis=1)
    got = lax.all_to_all(sent, "ctx", split_axis=0, concat_axis=2, tiled=True)[0]
    x_ctx = got[:channels]
    og = got[channels:]
    rows = sub * length // LANES
    taps_c = lax.dynamic_slice_in_dim(conv_taps[0], ctx * channels, channels, 2)
    taps_c = jnp.moveaxis(taps_c.reshape(3, 7, sec_n, sub), 2, 0).reshape(sec_n, 21 * sub)
    taps_c = exact_pieces(taps_c)
    taps_c = jnp.pad(taps_c, ((0, 0), (0, LANES - taps_c.shape[1])))
    sent = jnp.concatenate(
        [
            x_ctx.reshape(sec_n, rows, LANES),
            filters[0].reshape(sec_n, rows, LANES),
            taps_c[:, None, :],
        ],
        axis=1,
    )
    got = lax.all_to_all(sent, "section", split_axis=0, concat_axis=0, tiled=True)
    x_all = got[:, :rows]
    h_all = got[:, rows:2 * rows]
    taps_all = joined(got[:, 2 * rows, :63 * sub]).reshape(sec_n, 3, 7, sub)
    in_all, filter_grad, tap_grad = run_chain(x_all, h_all, og, taps_all)
    fg_high, fg_low = split_table(filter_grad.reshape(sec_n, span))
    sent = jnp.concatenate(
        [fg_high, fg_low, in_all.reshape(sec_n, span), exact_pieces(tap_grad.reshape(sec_n, 21 * sub))],
        axis=1,
    )
    got = lax.all_to_all(sent, "section", split_axis=0, concat_axis=0, tiled=True)
    fg = got[:, :span].astype(jnp.float32) + got[:, span:2 * span].astype(jnp.float32)
    fg = fg.reshape(1, channels, length)
    ig = got[:, 2 * span:3 * span].reshape(channels, length)
    tg = jnp.moveaxis(joined(got[:, 3 * span:]).reshape(sec_n, 3, 7, sub), 0, 2)
    tg = tg.reshape(1, 3, 7, channels)
    ig = lax.all_to_all(ig, "ctx", split_axis=1, concat_axis=0, tiled=True)
    return (ig[None], fg, tg)


def solution(mesh):
    placed = (
        P("section", None, "ctx"),
        P(None, "ctx"),
        P("section", "ctx", None),
        P("section", None, None, None),
    )
    return jax.shard_map(
        shards,
        mesh=mesh,
        in_specs=placed,
        out_specs=(
            P("section", None, "ctx"),
            P("section", "ctx", None),
            P("section", None, None, "ctx"),
        ),
        check_vma=False,
    )
```

```python
import math

import jax
import jax.numpy as jnp
from jax import lax
from jax.experimental import pallas as pl
from jax.experimental.pallas import tpu as pltpu
from jax.sharding import PartitionSpec as P

LANES = 128


def angle_table(row_count, col_count, modulus):
    row_ids = lax.broadcasted_iota(jnp.int32, (row_count, col_count), 0)
    col_ids = lax.broadcasted_iota(jnp.int32, (row_count, col_count), 1)
    product_mod = row_ids * col_ids % modulus
    angles = product_mod.astype(jnp.float32) * (2.0 * math.pi / modulus)
    return (jnp.cos(angles), jnp.sin(angles))


def split_bf16(value):
    high = value.astype(jnp.bfloat16)
    low = (value - high.astype(jnp.float32)).astype(jnp.bfloat16)
    return high, low


def split_table(value):
    high = lax.reduce_precision(value, exponent_bits=8, mantissa_bits=7)
    return high.astype(jnp.bfloat16), (value - high).astype(jnp.bfloat16)


def mat(a, b):
    return jnp.dot(a, b, preferred_element_type=jnp.float32)


def dot_left(t_hi, t_lo, value):
    v_hi, v_lo = split_bf16(value)
    return mat(t_hi, v_hi) + mat(t_hi, v_lo) + mat(t_lo, v_hi)


def dot_right(value, t_hi, t_lo):
    v_hi, v_lo = split_bf16(value)
    return mat(v_hi, t_hi) + mat(v_lo, t_hi) + mat(v_hi, t_lo)


def spectrum_tables(length):
    half = length // LANES
    blocks = 2 * half
    total = blocks * LANES
    cos_one, sin_one = angle_table(blocks, half, blocks)
    cos_tw, sin_tw = angle_table(blocks, LANES, total)
    cos_two, sin_two = angle_table(LANES, LANES, LANES)
    first = jnp.concatenate([cos_one, -sin_one], axis=0)
    forward = jnp.concatenate(
        [jnp.concatenate([cos_two, -sin_two], 1), jnp.concatenate([sin_two, cos_two], 1)], 0
    )
    backward = jnp.concatenate(
        [jnp.concatenate([cos_two, sin_two], 1), jnp.concatenate([-sin_two, cos_two], 1)], 0
    )
    last = jnp.concatenate([cos_one.T, -sin_one.T], axis=1) / total
    return (
        *split_table(first),
        cos_tw,
        sin_tw,
        *split_table(forward),
        *split_table(backward),
        *split_table(last),
    )


def chain_kernel(
    sub, taps_ref, x_ref, h_ref, og_ref, a1h, a1l, tcr, tsr, w2h, w2l, wbh, wbl, a3h, a3l,
    in_ref, fg_ref, tp_ref, q_s, k_s, v_s, conv_s, hs_s, ws_s, ds_s,
):
    layers, rows, lanes = x_ref.shape
    half = rows // sub
    blocks = 2 * half
    row_id = lax.broadcasted_iota(jnp.int32, (rows, lanes), 0)
    lane_id = lax.broadcasted_iota(jnp.int32, (rows, lanes), 1)
    first_row = row_id == 0
    last_row = row_id == half - 1
    for c in range(1, sub):
        first_row = first_row | (row_id == c * half)
        last_row = last_row | (row_id == c * half + half - 1)

    def fft(signal):
        twc = tcr[...]
        tws = tsr[...]
        parts = []
        for c in range(sub):
            y = dot_left(a1h[...], a1l[...], signal[c * half:(c + 1) * half, :])
            yr, yi = y[:blocks], y[blocks:]
            parts.append(jnp.concatenate([yr * twc + yi * tws, yi * twc - yr * tws], axis=1))
        return dot_right(jnp.concatenate(parts, axis=0), w2h[...], w2l[...])

    def ifft(spec):
        twc = tcr[...]
        tws = tsr[...]
        p = dot_right(spec, wbh[...], wbl[...])
        outs = []
        for c in range(sub):
            pr = p[c * blocks:(c + 1) * blocks, :lanes]
            pi = p[c * blocks:(c + 1) * blocks, lanes:]
            q = jnp.concatenate([pr * twc - pi * tws, pr * tws + pi * twc], axis=0)
            outs.append(dot_left(a3h[...], a3l[...], q))
        return jnp.concatenate(outs, axis=0)

    def back(value, j):
        if j == 0:
            return value
        r1 = pltpu.roll(value, j, 1)
        r2 = pltpu.roll(r1, 1, 0)
        out = jnp.where(lane_id >= j, r1, r2)
        return jnp.where(first_row & (lane_id < j), 0.0, out)

    def ahead(value, j):
        if j == 0:
            return value
        r1 = pltpu.roll(value, lanes - j, 1)
        r2 = pltpu.roll(r1, rows - 1, 0)
        out = jnp.where(lane_id < lanes - j, r1, r2)
        return jnp.where(last_row & (lane_id >= lanes - j), 0.0, out)

    def tap(layer, i, j):
        base = ((layer * 3 + i) * 7 + j) * sub
        w = jnp.full((rows, lanes), taps_ref[base + sub - 1], jnp.float32)
        for c in range(sub - 2, -1, -1):
            w = jnp.where(row_id < (c + 1) * half, taps_ref[base + c], w)
        return w

    def real_imag(spec):
        return spec[:, :lanes], spec[:, lanes:]

    def phase_one(layer, carry):
        x = x_ref[layer].astype(jnp.float32)
        feats = [jnp.zeros((rows, lanes), jnp.float32) for _ in range(3)]
        for j in range(7):
            xs = back(x, j)
            for i in range(3):
                feats[i] = feats[i] + tap(layer, i, j) * xs
        q, k, v = [f.astype(jnp.bfloat16).astype(jnp.float32) for f in feats]
        q_s[layer] = q
        k_s[layer] = k
        v_s[layer] = v
        hspec = fft(h_ref[layer].astype(jnp.float32))
        wspec = fft(k * v)
        hs_s[layer] = hspec
        ws_s[layer] = wspec
        hr, hi = real_imag(hspec)
        wr, wi = real_imag(wspec)
        conv_s[layer] = ifft(jnp.concatenate([hr * wr - hi * wi, hr * wi + hi * wr], axis=1))
        return carry

    lax.fori_loop(0, layers, phase_one, 0)

    def phase_two(step, carried):
        layer = layers - 1 - step
        grad_z = carried * q_s[layer]
        grad_q = carried * conv_s[layer]
        dspec = fft(grad_z)
        ds_s[layer] = dspec
        hr, hi = real_imag(hs_s[layer])
        dr, di = real_imag(dspec)
        grad_w = ifft(jnp.concatenate([hr * dr + hi * di, hr * di - hi * dr], axis=1))
        grads = (grad_q, grad_w * v_s[layer], grad_w * k_s[layer])
        summed = jnp.zeros((rows, lanes), jnp.float32)
        for j in range(7):
            term = tap(layer, 0, j) * grads[0]
            term = term + tap(layer, 1, j) * grads[1]
            term = term + tap(layer, 2, j) * grads[2]
            summed = summed + ahead(term, j)
        rounded = summed.astype(jnp.bfloat16)
        in_ref[layer] = rounded
        x = x_ref[layer].astype(jnp.float32)
        for j in range(7):
            xs = back(x, j)
            for i in range(3):
                prod = grads[i] * xs
                for c in range(sub):
                    row = (i * 7 + j) * sub + c
                    part = prod[c * half:c * half + 8, :]
                    for r in range(c * half + 8, (c + 1) * half, 8):
                        part = part + prod[r:r + 8, :]
                    tp_ref[layer, row] = part
        return rounded.astype(jnp.float32)

    lax.fori_loop(0, layers, phase_two, og_ref[...].astype(jnp.float32))

    def phase_three(layer, carry):
        wr, wi = real_imag(ws_s[layer])
        dr, di = real_imag(ds_s[layer])
        fg_ref[layer] = ifft(jnp.concatenate([wr * dr + wi * di, wr * di - wi * dr], axis=1))
        return carry

    lax.fori_loop(0, layers, phase_three, 0)


def run_chain(x_all, h_all, og, taps_all):
    layers, rows, _ = x_all.shape
    sub = taps_all.shape[3]
    half = rows // sub
    length = half * LANES
    blocks = 2 * half
    tables = spectrum_tables(length)
    vmem = pl.BlockSpec(memory_space=pltpu.VMEM)
    spec_shape = pltpu.VMEM((layers, sub * blocks, 2 * LANES), jnp.float32)
    sig_shape = pltpu.VMEM((layers, rows, LANES), jnp.float32)
    in_k, fg_k, tp_k = pl.pallas_call(
        lambda *refs: chain_kernel(sub, *refs),
        out_shape=(
            jax.ShapeDtypeStruct((layers, rows, LANES), jnp.bfloat16),
            jax.ShapeDtypeStruct((layers, rows, LANES), jnp.float32),
            jax.ShapeDtypeStruct((layers, 21 * sub, 8, LANES), jnp.float32),
        ),
        in_specs=[pl.BlockSpec(memory_space=pltpu.SMEM)] + [vmem] * 13,
        out_specs=(vmem, vmem, vmem),
        scratch_shapes=[sig_shape] * 4 + [spec_shape] * 3,
        compiler_params=pltpu.CompilerParams(vmem_limit_bytes=48 * 1024 * 1024),
        name="hyena_chain",
    )(
        taps_all.reshape(-1),
        x_all,
        h_all,
        og.reshape(rows, LANES),
        *tables,
    )
    tap_grad = jnp.sum(tp_k, axis=(2, 3)).reshape(layers, 3, 7, sub)
    return in_k.reshape(layers, sub, length), fg_k.reshape(layers, sub, length), tap_grad


def exact_pieces(value):
    pieces = []
    rest = value
    for _ in range(3):
        high = lax.reduce_precision(rest, exponent_bits=8, mantissa_bits=7)
        pieces.append(high.astype(jnp.bfloat16))
        rest = rest - high
    return jnp.concatenate(pieces, axis=-1)


def joined(pieces):
    third = pieces.shape[-1] // 3
    parts = [pieces[..., i * third:(i + 1) * third].astype(jnp.float32) for i in range(3)]
    return parts[0] + parts[1] + parts[2]


def shards(inputs, out_grad, filters, conv_taps):
    sec_n = lax.axis_size("section")
    ctx_n = lax.axis_size("ctx")
    sec = lax.axis_index("section")
    ctx = lax.axis_index("ctx")
    channels = filters.shape[1]
    length = filters.shape[2]
    sub = channels // sec_n
    tok_dev = inputs.shape[2]
    span = sub * length
    og = lax.dynamic_index_in_dim(
        out_grad.reshape(ctx_n, sec_n, sub, tok_dev), sec, 1, keepdims=False
    )
    sent = jnp.concatenate([inputs[0].reshape(ctx_n, channels, tok_dev), og], axis=1)
    got = lax.all_to_all(sent, "ctx", split_axis=0, concat_axis=2, tiled=True)[0]
    x_ctx = got[:channels]
    og = got[channels:]
    rows = sub * length // LANES
    taps_c = lax.dynamic_slice_in_dim(conv_taps[0], ctx * channels, channels, 2)
    taps_c = jnp.moveaxis(taps_c.reshape(3, 7, sec_n, sub), 2, 0).reshape(sec_n, 21 * sub)
    taps_c = exact_pieces(taps_c)
    taps_c = jnp.pad(taps_c, ((0, 0), (0, LANES - taps_c.shape[1])))
    sent = jnp.concatenate(
        [
            x_ctx.reshape(sec_n, rows, LANES),
            filters[0].reshape(sec_n, rows, LANES),
            taps_c[:, None, :],
        ],
        axis=1,
    )
    got = lax.all_to_all(sent, "section", split_axis=0, concat_axis=0, tiled=True)
    x_all = got[:, :rows]
    h_all = got[:, rows:2 * rows]
    taps_all = joined(got[:, 2 * rows, :63 * sub]).reshape(sec_n, 3, 7, sub)
    in_all, filter_grad, tap_grad = run_chain(x_all, h_all, og, taps_all)
    fg_high, fg_low = split_table(filter_grad.reshape(sec_n, span))
    sent = jnp.concatenate(
        [fg_high, fg_low, in_all.reshape(sec_n, span), exact_pieces(tap_grad.reshape(sec_n, 21 * sub))],
        axis=1,
    )
    got = lax.all_to_all(sent, "section", split_axis=0, concat_axis=0, tiled=True)
    fg = got[:, :span].astype(jnp.float32) + got[:, span:2 * span].astype(jnp.float32)
    fg = fg.reshape(1, channels, length)
    ig = got[:, 2 * span:3 * span].reshape(channels, length)
    tg = jnp.moveaxis(joined(got[:, 3 * span:]).reshape(sec_n, 3, 7, sub), 0, 2)
    tg = tg.reshape(1, 3, 7, channels)
    ig = lax.all_to_all(ig, "ctx", split_axis=1, concat_axis=0, tiled=True)
    return (ig[None], fg, tg)


def solution(mesh):
    placed = (
        P("section", None, "ctx"),
        P(None, "ctx"),
        P("section", "ctx", None),
        P("section", None, None, None),
    )
    return jax.shard_map(
        shards,
        mesh=mesh,
        in_specs=placed,
        out_specs=(
            P("section", None, "ctx"),
            P("section", "ctx", None),
            P("section", None, None, "ctx"),
        ),
        check_vma=False,
    )
```

```python
import math

import jax
import jax.numpy as jnp
from jax import lax
from jax.experimental import pallas as pl
from jax.experimental.pallas import tpu as pltpu
from jax.sharding import PartitionSpec as P

LANES = 128


def angle_table(row_count, col_count, modulus):
    row_ids = lax.broadcasted_iota(jnp.int32, (row_count, col_count), 0)
    col_ids = lax.broadcasted_iota(jnp.int32, (row_count, col_count), 1)
    product_mod = row_ids * col_ids % modulus
    angles = product_mod.astype(jnp.float32) * (2.0 * math.pi / modulus)
    return (jnp.cos(angles), jnp.sin(angles))


def split_bf16(value):
    high = value.astype(jnp.bfloat16)
    low = (value - high.astype(jnp.float32)).astype(jnp.bfloat16)
    return high, low


def split_table(value):
    high = lax.reduce_precision(value, exponent_bits=8, mantissa_bits=7)
    return high.astype(jnp.bfloat16), (value - high).astype(jnp.bfloat16)


def mat(a, b):
    return jnp.dot(a, b, preferred_element_type=jnp.float32)


def dot_left(t_hi, t_lo, value):
    v_hi, v_lo = split_bf16(value)
    return mat(t_hi, v_hi) + mat(t_hi, v_lo) + mat(t_lo, v_hi)


def dot_right(value, t_hi, t_lo):
    v_hi, v_lo = split_bf16(value)
    return mat(v_hi, t_hi) + mat(v_lo, t_hi) + mat(v_hi, t_lo)


def spectrum_tables(length):
    half = length // LANES
    blocks = 2 * half
    total = blocks * LANES
    cos_one, sin_one = angle_table(blocks, half, blocks)
    cos_tw, sin_tw = angle_table(blocks, LANES, total)
    cos_two, sin_two = angle_table(LANES, LANES, LANES)
    first = jnp.concatenate([cos_one, -sin_one], axis=0)
    forward = jnp.concatenate(
        [jnp.concatenate([cos_two, -sin_two], 1), jnp.concatenate([sin_two, cos_two], 1)], 0
    )
    backward = jnp.concatenate(
        [jnp.concatenate([cos_two, sin_two], 1), jnp.concatenate([-sin_two, cos_two], 1)], 0
    )
    last = jnp.concatenate([cos_one.T, -sin_one.T], axis=1) / total
    return (
        *split_table(first),
        cos_tw,
        sin_tw,
        *split_table(forward),
        *split_table(backward),
        *split_table(last),
    )


def chain_kernel(
    sub, taps_ref, x_ref, h_ref, og_ref, a1h, a1l, tcr, tsr, w2h, w2l, wbh, wbl, a3h, a3l,
    in_ref, fg_ref, tp_ref, q_s, k_s, v_s, conv_s, hs_s, ws_s, ds_s,
):
    layers, rows, lanes = x_ref.shape
    half = rows // sub
    blocks = 2 * half
    row_id = lax.broadcasted_iota(jnp.int32, (rows, lanes), 0)
    lane_id = lax.broadcasted_iota(jnp.int32, (rows, lanes), 1)
    first_row = row_id == 0
    last_row = row_id == half - 1
    for c in range(1, sub):
        first_row = first_row | (row_id == c * half)
        last_row = last_row | (row_id == c * half + half - 1)

    def fft(signal):
        twc = tcr[...]
        tws = tsr[...]
        parts = []
        for c in range(sub):
            y = dot_left(a1h[...], a1l[...], signal[c * half:(c + 1) * half, :])
            yr, yi = y[:blocks], y[blocks:]
            parts.append(jnp.concatenate([yr * twc + yi * tws, yi * twc - yr * tws], axis=1))
        return dot_right(jnp.concatenate(parts, axis=0), w2h[...], w2l[...])

    def ifft(spec):
        twc = tcr[...]
        tws = tsr[...]
        p = dot_right(spec, wbh[...], wbl[...])
        outs = []
        for c in range(sub):
            pr = p[c * blocks:(c + 1) * blocks, :lanes]
            pi = p[c * blocks:(c + 1) * blocks, lanes:]
            q = jnp.concatenate([pr * twc - pi * tws, pr * tws + pi * twc], axis=0)
            outs.append(dot_left(a3h[...], a3l[...], q))
        return jnp.concatenate(outs, axis=0)

    def back(value, j):
        if j == 0:
            return value
        r1 = pltpu.roll(value, j, 1)
        r2 = pltpu.roll(r1, 1, 0)
        out = jnp.where(lane_id >= j, r1, r2)
        return jnp.where(first_row & (lane_id < j), 0.0, out)

    def ahead(value, j):
        if j == 0:
            return value
        r1 = pltpu.roll(value, lanes - j, 1)
        r2 = pltpu.roll(r1, rows - 1, 0)
        out = jnp.where(lane_id < lanes - j, r1, r2)
        return jnp.where(last_row & (lane_id >= lanes - j), 0.0, out)

    def tap(layer, i, j):
        base = ((layer * 3 + i) * 7 + j) * sub
        w = jnp.full((rows, lanes), taps_ref[base + sub - 1], jnp.float32)
        for c in range(sub - 2, -1, -1):
            w = jnp.where(row_id < (c + 1) * half, taps_ref[base + c], w)
        return w

    def real_imag(spec):
        return spec[:, :lanes], spec[:, lanes:]

    def phase_one(layer, carry):
        x = x_ref[layer].astype(jnp.float32)
        feats = [jnp.zeros((rows, lanes), jnp.float32) for _ in range(3)]
        for j in range(7):
            xs = back(x, j)
            for i in range(3):
                feats[i] = feats[i] + tap(layer, i, j) * xs
        q, k, v = [f.astype(jnp.bfloat16).astype(jnp.float32) for f in feats]
        q_s[layer] = q
        k_s[layer] = k
        v_s[layer] = v
        hspec = fft(h_ref[layer].astype(jnp.float32))
        wspec = fft(k * v)
        hs_s[layer] = hspec
        ws_s[layer] = wspec
        hr, hi = real_imag(hspec)
        wr, wi = real_imag(wspec)
        conv_s[layer] = ifft(jnp.concatenate([hr * wr - hi * wi, hr * wi + hi * wr], axis=1))
        return carry

    lax.fori_loop(0, layers, phase_one, 0)

    def phase_two(step, carried):
        layer = layers - 1 - step
        grad_z = carried * q_s[layer]
        grad_q = carried * conv_s[layer]
        dspec = fft(grad_z)
        ds_s[layer] = dspec
        hr, hi = real_imag(hs_s[layer])
        dr, di = real_imag(dspec)
        grad_w = ifft(jnp.concatenate([hr * dr + hi * di, hr * di - hi * dr], axis=1))
        grads = (grad_q, grad_w * v_s[layer], grad_w * k_s[layer])
        summed = jnp.zeros((rows, lanes), jnp.float32)
        for j in range(7):
            term = tap(layer, 0, j) * grads[0]
            term = term + tap(layer, 1, j) * grads[1]
            term = term + tap(layer, 2, j) * grads[2]
            summed = summed + ahead(term, j)
        rounded = summed.astype(jnp.bfloat16)
        in_ref[layer] = rounded
        x = x_ref[layer].astype(jnp.float32)
        for j in range(7):
            xs = back(x, j)
            for i in range(3):
                prod = grads[i] * xs
                for c in range(sub):
                    row = (i * 7 + j) * sub + c
                    part = prod[c * half:c * half + 8, :]
                    for r in range(c * half + 8, (c + 1) * half, 8):
                        part = part + prod[r:r + 8, :]
                    tp_ref[layer, row] = part
        return rounded.astype(jnp.float32)

    lax.fori_loop(0, layers, phase_two, og_ref[...].astype(jnp.float32))

    def phase_three(layer, carry):
        wr, wi = real_imag(ws_s[layer])
        dr, di = real_imag(ds_s[layer])
        fg_ref[layer] = ifft(jnp.concatenate([wr * dr + wi * di, wr * di - wi * dr], axis=1))
        return carry

    lax.fori_loop(0, layers, phase_three, 0)


def run_chain(x_all, h_all, og, taps_all):
    layers, rows, _ = x_all.shape
    sub = taps_all.shape[3]
    half = rows // sub
    length = half * LANES
    blocks = 2 * half
    tables = spectrum_tables(length)
    vmem = pl.BlockSpec(memory_space=pltpu.VMEM)
    spec_shape = pltpu.VMEM((layers, sub * blocks, 2 * LANES), jnp.float32)
    sig_shape = pltpu.VMEM((layers, rows, LANES), jnp.float32)
    in_k, fg_k, tp_k = pl.pallas_call(
        lambda *refs: chain_kernel(sub, *refs),
        out_shape=(
            jax.ShapeDtypeStruct((layers, rows, LANES), jnp.bfloat16),
            jax.ShapeDtypeStruct((layers, rows, LANES), jnp.float32),
            jax.ShapeDtypeStruct((layers, 21 * sub, 8, LANES), jnp.float32),
        ),
        in_specs=[pl.BlockSpec(memory_space=pltpu.SMEM)] + [vmem] * 13,
        out_specs=(vmem, vmem, vmem),
        scratch_shapes=[sig_shape] * 4 + [spec_shape] * 3,
        compiler_params=pltpu.CompilerParams(vmem_limit_bytes=48 * 1024 * 1024),
        name="hyena_chain",
    )(
        taps_all.reshape(-1),
        x_all,
        h_all,
        og.reshape(rows, LANES),
        *tables,
    )
    tap_grad = jnp.sum(tp_k, axis=(2, 3)).reshape(layers, 3, 7, sub)
    return in_k.reshape(layers, sub, length), fg_k.reshape(layers, sub, length), tap_grad


def exact_pieces(value):
    pieces = []
    rest = value
    for _ in range(3):
        high = lax.reduce_precision(rest, exponent_bits=8, mantissa_bits=7)
        pieces.append(high.astype(jnp.bfloat16))
        rest = rest - high
    return jnp.concatenate(pieces, axis=-1)


def joined(pieces):
    third = pieces.shape[-1] // 3
    parts = [pieces[..., i * third:(i + 1) * third].astype(jnp.float32) for i in range(3)]
    return parts[0] + parts[1] + parts[2]


def shards(inputs, out_grad, filters, conv_taps):
    sec_n = lax.axis_size("section")
    ctx_n = lax.axis_size("ctx")
    sec = lax.axis_index("section")
    ctx = lax.axis_index("ctx")
    channels = filters.shape[1]
    length = filters.shape[2]
    sub = channels // sec_n
    tok_dev = inputs.shape[2]
    span = sub * length
    og = lax.dynamic_index_in_dim(
        out_grad.reshape(ctx_n, sec_n, sub, tok_dev), sec, 1, keepdims=False
    )
    sent = jnp.concatenate([inputs[0].reshape(ctx_n, channels, tok_dev), og], axis=1)
    got = lax.all_to_all(sent, "ctx", split_axis=0, concat_axis=2, tiled=True)[0]
    x_ctx = got[:channels]
    og = got[channels:]
    rows = sub * length // LANES
    taps_c = lax.dynamic_slice_in_dim(conv_taps[0], ctx * channels, channels, 2)
    taps_c = jnp.moveaxis(taps_c.reshape(3, 7, sec_n, sub), 2, 0).reshape(sec_n, 21 * sub)
    taps_c = exact_pieces(taps_c)
    taps_c = jnp.pad(taps_c, ((0, 0), (0, LANES - taps_c.shape[1])))
    sent = jnp.concatenate(
        [
            x_ctx.reshape(sec_n, rows, LANES),
            filters[0].reshape(sec_n, rows, LANES),
            taps_c[:, None, :],
        ],
        axis=1,
    )
    got = lax.all_to_all(sent, "section", split_axis=0, concat_axis=0, tiled=True)
    x_all = got[:, :rows]
    h_all = got[:, rows:2 * rows]
    taps_all = joined(got[:, 2 * rows, :63 * sub]).reshape(sec_n, 3, 7, sub)
    in_all, filter_grad, tap_grad = run_chain(x_all, h_all, og, taps_all)
    fg_high, fg_low = split_table(filter_grad.reshape(sec_n, span))
    taps_out = exact_pieces(tap_grad.reshape(sec_n, 21 * sub))
    taps_out = jnp.pad(taps_out, ((0, 0), (0, LANES - taps_out.shape[1])))
    sent = jnp.concatenate(
        [fg_high, fg_low, in_all.reshape(sec_n, span), taps_out],
        axis=1,
    )
    got = lax.all_to_all(
        sent.reshape(sec_n, -1, LANES), "section", split_axis=0, concat_axis=0, tiled=True
    ).reshape(sec_n, -1)
    fg = got[:, :span].astype(jnp.float32) + got[:, span:2 * span].astype(jnp.float32)
    fg = fg.reshape(1, channels, length)
    ig = got[:, 2 * span:3 * span].reshape(channels, length)
    tg = jnp.moveaxis(joined(got[:, 3 * span:3 * span + 63 * sub]).reshape(sec_n, 3, 7, sub), 0, 2)
    tg = tg.reshape(1, 3, 7, channels)
    ig = lax.all_to_all(ig, "ctx", split_axis=1, concat_axis=0, tiled=True)
    return (ig[None], fg, tg)


def solution(mesh):
    placed = (
        P("section", None, "ctx"),
        P(None, "ctx"),
        P("section", "ctx", None),
        P("section", None, None, None),
    )
    return jax.shard_map(
        shards,
        mesh=mesh,
        in_specs=placed,
        out_specs=(
            P("section", None, "ctx"),
            P("section", "ctx", None),
            P("section", None, None, "ctx"),
        ),
        check_vma=False,
    )
```

```python
import math

import jax
import jax.numpy as jnp
from jax import lax
from jax.experimental import pallas as pl
from jax.experimental.pallas import tpu as pltpu
from jax.sharding import PartitionSpec as P

LANES = 128


def angle_table(row_count, col_count, modulus):
    row_ids = lax.broadcasted_iota(jnp.int32, (row_count, col_count), 0)
    col_ids = lax.broadcasted_iota(jnp.int32, (row_count, col_count), 1)
    product_mod = row_ids * col_ids % modulus
    angles = product_mod.astype(jnp.float32) * (2.0 * math.pi / modulus)
    return (jnp.cos(angles), jnp.sin(angles))


def split_bf16(value):
    high = value.astype(jnp.bfloat16)
    low = (value - high.astype(jnp.float32)).astype(jnp.bfloat16)
    return high, low


def split_table(value):
    high = lax.reduce_precision(value, exponent_bits=8, mantissa_bits=7)
    return high.astype(jnp.bfloat16), (value - high).astype(jnp.bfloat16)


def mat(a, b):
    return jnp.dot(a, b, preferred_element_type=jnp.float32)


def dot_left(t_hi, t_lo, value):
    v_hi, v_lo = split_bf16(value)
    return mat(t_hi, v_hi) + mat(t_hi, v_lo) + mat(t_lo, v_hi)


def dot_right(value, t_hi, t_lo):
    v_hi, v_lo = split_bf16(value)
    return mat(v_hi, t_hi) + mat(v_lo, t_hi) + mat(v_hi, t_lo)


def spectrum_tables(length):
    half = length // LANES
    blocks = 2 * half
    total = blocks * LANES
    cos_one, sin_one = angle_table(blocks, half, blocks)
    cos_tw, sin_tw = angle_table(blocks, LANES, total)
    cos_two, sin_two = angle_table(LANES, LANES, LANES)
    first = jnp.concatenate([cos_one, -sin_one], axis=0)
    forward = jnp.concatenate(
        [jnp.concatenate([cos_two, -sin_two], 1), jnp.concatenate([sin_two, cos_two], 1)], 0
    )
    backward = jnp.concatenate(
        [jnp.concatenate([cos_two, sin_two], 1), jnp.concatenate([-sin_two, cos_two], 1)], 0
    )
    last = jnp.concatenate([cos_one.T, -sin_one.T], axis=1) / total
    return (
        *split_table(first),
        cos_tw,
        sin_tw,
        *split_table(forward),
        *split_table(backward),
        *split_table(last),
    )


def chain_kernel(
    sub, taps_ref, x_ref, h_ref, og_ref, a1h, a1l, tcr, tsr, w2h, w2l, wbh, wbl, a3h, a3l,
    in_ref, fg_ref, tp_ref, q_s, k_s, v_s, conv_s, hs_s, ws_s, ds_s,
):
    layers, rows, lanes = x_ref.shape
    half = rows // sub
    blocks = 2 * half
    row_id = lax.broadcasted_iota(jnp.int32, (rows, lanes), 0)
    lane_id = lax.broadcasted_iota(jnp.int32, (rows, lanes), 1)
    first_row = row_id == 0
    last_row = row_id == half - 1
    for c in range(1, sub):
        first_row = first_row | (row_id == c * half)
        last_row = last_row | (row_id == c * half + half - 1)

    def fft(signal):
        twc = tcr[...]
        tws = tsr[...]
        parts = []
        for c in range(sub):
            y = dot_left(a1h[...], a1l[...], signal[c * half:(c + 1) * half, :])
            yr, yi = y[:blocks], y[blocks:]
            parts.append(jnp.concatenate([yr * twc + yi * tws, yi * twc - yr * tws], axis=1))
        return dot_right(jnp.concatenate(parts, axis=0), w2h[...], w2l[...])

    def ifft(spec):
        twc = tcr[...]
        tws = tsr[...]
        p = dot_right(spec, wbh[...], wbl[...])
        outs = []
        for c in range(sub):
            pr = p[c * blocks:(c + 1) * blocks, :lanes]
            pi = p[c * blocks:(c + 1) * blocks, lanes:]
            q = jnp.concatenate([pr * twc - pi * tws, pr * tws + pi * twc], axis=0)
            outs.append(dot_left(a3h[...], a3l[...], q))
        return jnp.concatenate(outs, axis=0)

    def back(value, j):
        if j == 0:
            return value
        r1 = pltpu.roll(value, j, 1)
        r2 = pltpu.roll(r1, 1, 0)
        out = jnp.where(lane_id >= j, r1, r2)
        return jnp.where(first_row & (lane_id < j), 0.0, out)

    def ahead(value, j):
        if j == 0:
            return value
        r1 = pltpu.roll(value, lanes - j, 1)
        r2 = pltpu.roll(r1, rows - 1, 0)
        out = jnp.where(lane_id < lanes - j, r1, r2)
        return jnp.where(last_row & (lane_id >= lanes - j), 0.0, out)

    def tap(layer, i, j):
        base = ((layer * 3 + i) * 7 + j) * sub
        w = jnp.full((rows, lanes), taps_ref[base + sub - 1], jnp.float32)
        for c in range(sub - 2, -1, -1):
            w = jnp.where(row_id < (c + 1) * half, taps_ref[base + c], w)
        return w

    def real_imag(spec):
        return spec[:, :lanes], spec[:, lanes:]

    def phase_one(layer, carry):
        x = x_ref[layer].astype(jnp.float32)
        feats = [jnp.zeros((rows, lanes), jnp.float32) for _ in range(3)]
        for j in range(7):
            xs = back(x, j)
            for i in range(3):
                feats[i] = feats[i] + tap(layer, i, j) * xs
        q, k, v = [f.astype(jnp.bfloat16).astype(jnp.float32) for f in feats]
        q_s[layer] = q
        k_s[layer] = k
        v_s[layer] = v
        hspec = fft(h_ref[layer].astype(jnp.float32))
        wspec = fft(k * v)
        hs_s[layer] = hspec
        ws_s[layer] = wspec
        hr, hi = real_imag(hspec)
        wr, wi = real_imag(wspec)
        conv_s[layer] = ifft(jnp.concatenate([hr * wr - hi * wi, hr * wi + hi * wr], axis=1))
        return carry

    lax.fori_loop(0, layers, phase_one, 0)

    def phase_two(step, carried):
        layer = layers - 1 - step
        grad_z = carried * q_s[layer]
        grad_q = carried * conv_s[layer]
        dspec = fft(grad_z)
        ds_s[layer] = dspec
        hr, hi = real_imag(hs_s[layer])
        dr, di = real_imag(dspec)
        grad_w = ifft(jnp.concatenate([hr * dr + hi * di, hr * di - hi * dr], axis=1))
        grads = (grad_q, grad_w * v_s[layer], grad_w * k_s[layer])
        summed = jnp.zeros((rows, lanes), jnp.float32)
        for j in range(7):
            term = tap(layer, 0, j) * grads[0]
            term = term + tap(layer, 1, j) * grads[1]
            term = term + tap(layer, 2, j) * grads[2]
            summed = summed + ahead(term, j)
        rounded = summed.astype(jnp.bfloat16)
        in_ref[layer] = rounded
        x = x_ref[layer].astype(jnp.float32)
        for j in range(7):
            xs = back(x, j)
            for i in range(3):
                prod = grads[i] * xs
                for c in range(sub):
                    row = (i * 7 + j) * sub + c
                    part = prod[c * half:c * half + 8, :]
                    for r in range(c * half + 8, (c + 1) * half, 8):
                        part = part + prod[r:r + 8, :]
                    tp_ref[layer, row] = part
        return rounded.astype(jnp.float32)

    lax.fori_loop(0, layers, phase_two, og_ref[...].astype(jnp.float32))

    def phase_three(layer, carry):
        wr, wi = real_imag(ws_s[layer])
        dr, di = real_imag(ds_s[layer])
        fg_ref[layer] = ifft(jnp.concatenate([wr * dr + wi * di, wr * di - wi * dr], axis=1))
        return carry

    lax.fori_loop(0, layers, phase_three, 0)


def run_chain(x_all, h_all, og, taps_all):
    layers, rows, _ = x_all.shape
    sub = taps_all.shape[3]
    half = rows // sub
    length = half * LANES
    blocks = 2 * half
    tables = spectrum_tables(length)
    vmem = pl.BlockSpec(memory_space=pltpu.VMEM)
    spec_shape = pltpu.VMEM((layers, sub * blocks, 2 * LANES), jnp.float32)
    sig_shape = pltpu.VMEM((layers, rows, LANES), jnp.float32)
    in_k, fg_k, tp_k = pl.pallas_call(
        lambda *refs: chain_kernel(sub, *refs),
        out_shape=(
            jax.ShapeDtypeStruct((layers, rows, LANES), jnp.bfloat16),
            jax.ShapeDtypeStruct((layers, rows, LANES), jnp.float32),
            jax.ShapeDtypeStruct((layers, 21 * sub, 8, LANES), jnp.float32),
        ),
        in_specs=[pl.BlockSpec(memory_space=pltpu.SMEM)] + [vmem] * 13,
        out_specs=(vmem, vmem, vmem),
        scratch_shapes=[sig_shape] * 4 + [spec_shape] * 3,
        compiler_params=pltpu.CompilerParams(vmem_limit_bytes=48 * 1024 * 1024),
        name="hyena_chain",
    )(
        taps_all.reshape(-1),
        x_all,
        h_all,
        og.reshape(rows, LANES),
        *tables,
    )
    tap_grad = jnp.sum(tp_k, axis=(2, 3)).reshape(layers, 3, 7, sub)
    return in_k.reshape(layers, sub, length), fg_k.reshape(layers, sub, length), tap_grad


def exact_pieces(value):
    pieces = []
    rest = value
    for _ in range(3):
        high = lax.reduce_precision(rest, exponent_bits=8, mantissa_bits=7)
        pieces.append(high.astype(jnp.bfloat16))
        rest = rest - high
    return jnp.concatenate(pieces, axis=-1)


def joined(pieces):
    third = pieces.shape[-1] // 3
    parts = [pieces[..., i * third:(i + 1) * third].astype(jnp.float32) for i in range(3)]
    return parts[0] + parts[1] + parts[2]


def shards(inputs, out_grad, filters, conv_taps):
    sec_n = lax.axis_size("section")
    ctx_n = lax.axis_size("ctx")
    sec = lax.axis_index("section")
    ctx = lax.axis_index("ctx")
    channels = filters.shape[1]
    length = filters.shape[2]
    sub = channels // sec_n
    tok_dev = inputs.shape[2]
    span = sub * length
    og = lax.dynamic_index_in_dim(
        out_grad.reshape(ctx_n, sec_n, sub, tok_dev), sec, 1, keepdims=False
    )
    sent = jnp.concatenate([inputs[0].reshape(ctx_n, channels, tok_dev), og], axis=1)
    got = lax.all_to_all(sent, "ctx", split_axis=0, concat_axis=2, tiled=True)[0]
    x_ctx = got[:channels]
    og = got[channels:]
    rows = sub * length // LANES
    taps_c = lax.dynamic_slice_in_dim(conv_taps[0], ctx * channels, channels, 2)
    taps_c = jnp.moveaxis(taps_c.reshape(3, 7, sec_n, sub), 2, 0).reshape(sec_n, 21 * sub)
    taps_c = exact_pieces(taps_c)
    taps_c = jnp.pad(taps_c, ((0, 0), (0, LANES - taps_c.shape[1])))
    sent = jnp.concatenate(
        [
            x_ctx.reshape(sec_n, rows, LANES),
            filters[0].reshape(sec_n, rows, LANES),
            taps_c[:, None, :],
        ],
        axis=1,
    )
    got = lax.all_to_all(sent, "section", split_axis=0, concat_axis=0, tiled=True)
    x_all = got[:, :rows]
    h_all = got[:, rows:2 * rows]
    taps_all = joined(got[:, 2 * rows, :63 * sub]).reshape(sec_n, 3, 7, sub)
    in_all, filter_grad, tap_grad = run_chain(x_all, h_all, og, taps_all)
    fg_high, fg_low = split_table(filter_grad.reshape(sec_n, span))
    taps_out = exact_pieces(tap_grad.reshape(sec_n, 21 * sub))
    taps_out = jnp.pad(taps_out, ((0, 0), (0, LANES - taps_out.shape[1])))
    sent = jnp.concatenate(
        [fg_high, fg_low, in_all.reshape(sec_n, span), taps_out],
        axis=1,
    )
    got3 = lax.all_to_all(
        sent.reshape(sec_n, -1, LANES), "section", split_axis=0, concat_axis=0, tiled=True
    )
    got = got3.reshape(sec_n, -1)
    fg = got[:, :span].astype(jnp.float32) + got[:, span:2 * span].astype(jnp.float32)
    fg = fg.reshape(1, channels, length)
    ig = got3[:, 2 * rows:3 * rows].reshape(sec_n, sub, ctx_n, tok_dev)
    ig = jnp.transpose(ig, (2, 0, 1, 3)).reshape(ctx_n, channels, tok_dev)
    tg = jnp.moveaxis(joined(got[:, 3 * span:3 * span + 63 * sub]).reshape(sec_n, 3, 7, sub), 0, 2)
    tg = tg.reshape(1, 3, 7, channels)
    ig = lax.all_to_all(ig, "ctx", split_axis=0, concat_axis=0, tiled=True)
    return (ig.reshape(1, ctx_n * channels, tok_dev), fg, tg)


def solution(mesh):
    placed = (
        P("section", None, "ctx"),
        P(None, "ctx"),
        P("section", "ctx", None),
        P("section", None, None, None),
    )
    return jax.shard_map(
        shards,
        mesh=mesh,
        in_specs=placed,
        out_specs=(
            P("section", None, "ctx"),
            P("section", "ctx", None),
            P("section", None, None, "ctx"),
        ),
        check_vma=False,
    )
```

```python
import math

import jax
import jax.numpy as jnp
from jax import lax
from jax.experimental import pallas as pl
from jax.experimental.pallas import tpu as pltpu
from jax.sharding import PartitionSpec as P

LANES = 128


def angle_table(row_count, col_count, modulus):
    row_ids = lax.broadcasted_iota(jnp.int32, (row_count, col_count), 0)
    col_ids = lax.broadcasted_iota(jnp.int32, (row_count, col_count), 1)
    product_mod = row_ids * col_ids % modulus
    angles = product_mod.astype(jnp.float32) * (2.0 * math.pi / modulus)
    return (jnp.cos(angles), jnp.sin(angles))


def split_bf16(value):
    high = value.astype(jnp.bfloat16)
    low = (value - high.astype(jnp.float32)).astype(jnp.bfloat16)
    return high, low


def split_table(value):
    high = lax.reduce_precision(value, exponent_bits=8, mantissa_bits=7)
    return high.astype(jnp.bfloat16), (value - high).astype(jnp.bfloat16)


def mat(a, b):
    return jnp.dot(a, b, preferred_element_type=jnp.float32)


def dot_left(t_hi, t_lo, value):
    v_hi, v_lo = split_bf16(value)
    return mat(t_hi, v_hi) + mat(t_hi, v_lo) + mat(t_lo, v_hi)


def dot_right(value, t_hi, t_lo):
    v_hi, v_lo = split_bf16(value)
    return mat(v_hi, t_hi) + mat(v_lo, t_hi) + mat(v_hi, t_lo)


def spectrum_tables(length):
    half = length // LANES
    blocks = 2 * half
    total = blocks * LANES
    cos_one, sin_one = angle_table(blocks, half, blocks)
    cos_tw, sin_tw = angle_table(blocks, LANES, total)
    cos_two, sin_two = angle_table(LANES, LANES, LANES)
    first = jnp.concatenate([cos_one, -sin_one], axis=0)
    forward = jnp.concatenate(
        [jnp.concatenate([cos_two, -sin_two], 1), jnp.concatenate([sin_two, cos_two], 1)], 0
    )
    backward = jnp.concatenate(
        [jnp.concatenate([cos_two, sin_two], 1), jnp.concatenate([-sin_two, cos_two], 1)], 0
    )
    last = jnp.concatenate([cos_one.T, -sin_one.T], axis=1) / total
    return (
        *split_table(first),
        cos_tw,
        sin_tw,
        *split_table(forward),
        *split_table(backward),
        *split_table(last),
    )


def chain_kernel(
    sub, taps_ref, x_ref, h_ref, og_ref, a1h, a1l, tcr, tsr, w2h, w2l, wbh, wbl, a3h, a3l,
    in_ref, fg_ref, tp_ref, q_s, k_s, v_s, conv_s, hs_s, ws_s, ds_s, xs_s,
):
    layers, rows, lanes = x_ref.shape
    half = rows // sub
    blocks = 2 * half
    row_id = lax.broadcasted_iota(jnp.int32, (rows, lanes), 0)
    lane_id = lax.broadcasted_iota(jnp.int32, (rows, lanes), 1)
    first_row = row_id == 0
    last_row = row_id == half - 1
    for c in range(1, sub):
        first_row = first_row | (row_id == c * half)
        last_row = last_row | (row_id == c * half + half - 1)

    def fft(signal, exact=False):
        twc = tcr[...]
        tws = tsr[...]
        parts = []
        for c in range(sub):
            piece = signal[c * half:(c + 1) * half, :]
            if exact:
                v_hi = piece.astype(jnp.bfloat16)
                y = mat(a1h[...], v_hi) + mat(a1l[...], v_hi)
            else:
                y = dot_left(a1h[...], a1l[...], piece)
            yr, yi = y[:blocks], y[blocks:]
            parts.append(jnp.concatenate([yr * twc + yi * tws, yi * twc - yr * tws], axis=1))
        return dot_right(jnp.concatenate(parts, axis=0), w2h[...], w2l[...])

    def ifft(spec):
        twc = tcr[...]
        tws = tsr[...]
        p = dot_right(spec, wbh[...], wbl[...])
        outs = []
        for c in range(sub):
            pr = p[c * blocks:(c + 1) * blocks, :lanes]
            pi = p[c * blocks:(c + 1) * blocks, lanes:]
            q = jnp.concatenate([pr * twc - pi * tws, pr * tws + pi * twc], axis=0)
            outs.append(dot_left(a3h[...], a3l[...], q))
        return jnp.concatenate(outs, axis=0)

    def back(value, j):
        if j == 0:
            return value
        r1 = pltpu.roll(value, j, 1)
        r2 = pltpu.roll(r1, 1, 0)
        out = jnp.where(lane_id >= j, r1, r2)
        return jnp.where(first_row & (lane_id < j), 0.0, out)

    def ahead(value, j):
        if j == 0:
            return value
        r1 = pltpu.roll(value, lanes - j, 1)
        r2 = pltpu.roll(r1, rows - 1, 0)
        out = jnp.where(lane_id < lanes - j, r1, r2)
        return jnp.where(last_row & (lane_id >= lanes - j), 0.0, out)

    def tap(layer, i, j):
        base = ((layer * 3 + i) * 7 + j) * sub
        w = jnp.full((rows, lanes), taps_ref[base + sub - 1], jnp.float32)
        for c in range(sub - 2, -1, -1):
            w = jnp.where(row_id < (c + 1) * half, taps_ref[base + c], w)
        return w

    def real_imag(spec):
        return spec[:, :lanes], spec[:, lanes:]

    def phase_one(layer, carry):
        x = x_ref[layer].astype(jnp.float32)
        feats = [jnp.zeros((rows, lanes), jnp.float32) for _ in range(3)]
        for j in range(7):
            xs = back(x, j)
            xs_s[layer * 7 + j] = xs
            for i in range(3):
                feats[i] = feats[i] + tap(layer, i, j) * xs
        q, k, v = [f.astype(jnp.bfloat16).astype(jnp.float32) for f in feats]
        q_s[layer] = q
        k_s[layer] = k
        v_s[layer] = v
        hspec = fft(h_ref[layer], exact=True)
        wspec = fft(k * v)
        hs_s[layer] = hspec
        ws_s[layer] = wspec
        hr, hi = real_imag(hspec)
        wr, wi = real_imag(wspec)
        conv_s[layer] = ifft(jnp.concatenate([hr * wr - hi * wi, hr * wi + hi * wr], axis=1))
        return carry

    lax.fori_loop(0, layers, phase_one, 0)

    def phase_two(step, carried):
        layer = layers - 1 - step
        grad_z = carried * q_s[layer]
        grad_q = carried * conv_s[layer]
        dspec = fft(grad_z)
        ds_s[layer] = dspec
        hr, hi = real_imag(hs_s[layer])
        dr, di = real_imag(dspec)
        grad_w = ifft(jnp.concatenate([hr * dr + hi * di, hr * di - hi * dr], axis=1))
        grads = (grad_q, grad_w * v_s[layer], grad_w * k_s[layer])
        summed = jnp.zeros((rows, lanes), jnp.float32)
        for j in range(7):
            term = tap(layer, 0, j) * grads[0]
            term = term + tap(layer, 1, j) * grads[1]
            term = term + tap(layer, 2, j) * grads[2]
            summed = summed + ahead(term, j)
        rounded = summed.astype(jnp.bfloat16)
        in_ref[layer] = rounded
        for j in range(7):
            xs = xs_s[layer * 7 + j]
            for i in range(3):
                prod = grads[i] * xs
                for c in range(sub):
                    row = (i * 7 + j) * sub + c
                    part = prod[c * half:c * half + 8, :]
                    for r in range(c * half + 8, (c + 1) * half, 8):
                        part = part + prod[r:r + 8, :]
                    tp_ref[layer, row] = part
        return rounded.astype(jnp.float32)

    lax.fori_loop(0, layers, phase_two, og_ref[...].astype(jnp.float32))

    def phase_three(layer, carry):
        wr, wi = real_imag(ws_s[layer])
        dr, di = real_imag(ds_s[layer])
        fg_ref[layer] = ifft(jnp.concatenate([wr * dr + wi * di, wr * di - wi * dr], axis=1))
        return carry

    lax.fori_loop(0, layers, phase_three, 0)


def run_chain(x_all, h_all, og, taps_all):
    layers, rows, _ = x_all.shape
    sub = taps_all.shape[3]
    half = rows // sub
    length = half * LANES
    blocks = 2 * half
    tables = spectrum_tables(length)
    vmem = pl.BlockSpec(memory_space=pltpu.VMEM)
    spec_shape = pltpu.VMEM((layers, sub * blocks, 2 * LANES), jnp.float32)
    sig_shape = pltpu.VMEM((layers, rows, LANES), jnp.float32)
    in_k, fg_k, tp_k = pl.pallas_call(
        lambda *refs: chain_kernel(sub, *refs),
        out_shape=(
            jax.ShapeDtypeStruct((layers, rows, LANES), jnp.bfloat16),
            jax.ShapeDtypeStruct((layers, rows, LANES), jnp.float32),
            jax.ShapeDtypeStruct((layers, 21 * sub, 8, LANES), jnp.float32),
        ),
        in_specs=[pl.BlockSpec(memory_space=pltpu.SMEM)] + [vmem] * 13,
        out_specs=(vmem, vmem, vmem),
        scratch_shapes=[sig_shape] * 4
        + [spec_shape] * 3
        + [pltpu.VMEM((layers * 7, rows, LANES), jnp.float32)],
        compiler_params=pltpu.CompilerParams(vmem_limit_bytes=48 * 1024 * 1024),
        name="hyena_chain",
    )(
        taps_all.reshape(-1),
        x_all,
        h_all,
        og.reshape(rows, LANES),
        *tables,
    )
    tap_grad = jnp.sum(tp_k, axis=(2, 3)).reshape(layers, 3, 7, sub)
    return in_k.reshape(layers, sub, length), fg_k.reshape(layers, sub, length), tap_grad


def exact_pieces(value):
    pieces = []
    rest = value
    for _ in range(3):
        high = lax.reduce_precision(rest, exponent_bits=8, mantissa_bits=7)
        pieces.append(high.astype(jnp.bfloat16))
        rest = rest - high
    return jnp.concatenate(pieces, axis=-1)


def joined(pieces):
    third = pieces.shape[-1] // 3
    parts = [pieces[..., i * third:(i + 1) * third].astype(jnp.float32) for i in range(3)]
    return parts[0] + parts[1] + parts[2]


def shards(inputs, out_grad, filters, conv_taps):
    sec_n = lax.axis_size("section")
    ctx_n = lax.axis_size("ctx")
    sec = lax.axis_index("section")
    ctx = lax.axis_index("ctx")
    channels = filters.shape[1]
    length = filters.shape[2]
    sub = channels // sec_n
    tok_dev = inputs.shape[2]
    span = sub * length
    og = lax.dynamic_index_in_dim(
        out_grad.reshape(ctx_n, sec_n, sub, tok_dev), sec, 1, keepdims=False
    )
    sent = jnp.concatenate([inputs[0].reshape(ctx_n, channels, tok_dev), og], axis=1)
    got = lax.all_to_all(sent, "ctx", split_axis=0, concat_axis=2, tiled=True)[0]
    x_ctx = got[:channels]
    og = got[channels:]
    rows = sub * length // LANES
    taps_c = lax.dynamic_slice_in_dim(conv_taps[0], ctx * channels, channels, 2)
    taps_c = jnp.moveaxis(taps_c.reshape(3, 7, sec_n, sub), 2, 0).reshape(sec_n, 21 * sub)
    taps_c = exact_pieces(taps_c)
    taps_c = jnp.pad(taps_c, ((0, 0), (0, LANES - taps_c.shape[1])))
    sent = jnp.concatenate(
        [
            x_ctx.reshape(sec_n, rows, LANES),
            filters[0].reshape(sec_n, rows, LANES),
            taps_c[:, None, :],
        ],
        axis=1,
    )
    got = lax.all_to_all(sent, "section", split_axis=0, concat_axis=0, tiled=True)
    x_all = got[:, :rows]
    h_all = got[:, rows:2 * rows]
    taps_all = joined(got[:, 2 * rows, :63 * sub]).reshape(sec_n, 3, 7, sub)
    in_all, filter_grad, tap_grad = run_chain(x_all, h_all, og, taps_all)
    fg_high, fg_low = split_table(filter_grad.reshape(sec_n, span))
    taps_out = exact_pieces(tap_grad.reshape(sec_n, 21 * sub))
    taps_out = jnp.pad(taps_out, ((0, 0), (0, LANES - taps_out.shape[1])))
    sent = jnp.concatenate(
        [fg_high, fg_low, in_all.reshape(sec_n, span), taps_out],
        axis=1,
    )
    got3 = lax.all_to_all(
        sent.reshape(sec_n, -1, LANES), "section", split_axis=0, concat_axis=0, tiled=True
    )
    got = got3.reshape(sec_n, -1)
    fg = got[:, :span].astype(jnp.float32) + got[:, span:2 * span].astype(jnp.float32)
    fg = fg.reshape(1, channels, length)
    ig = got3[:, 2 * rows:3 * rows].reshape(sec_n, sub, ctx_n, tok_dev)
    ig = jnp.transpose(ig, (2, 0, 1, 3)).reshape(ctx_n, channels, tok_dev)
    tg = jnp.moveaxis(joined(got[:, 3 * span:3 * span + 63 * sub]).reshape(sec_n, 3, 7, sub), 0, 2)
    tg = tg.reshape(1, 3, 7, channels)
    ig = lax.all_to_all(ig, "ctx", split_axis=0, concat_axis=0, tiled=True)
    return (ig.reshape(1, ctx_n * channels, tok_dev), fg, tg)


def solution(mesh):
    placed = (
        P("section", None, "ctx"),
        P(None, "ctx"),
        P("section", "ctx", None),
        P("section", None, None, None),
    )
    return jax.shard_map(
        shards,
        mesh=mesh,
        in_specs=placed,
        out_specs=(
            P("section", None, "ctx"),
            P("section", "ctx", None),
            P("section", None, None, "ctx"),
        ),
        check_vma=False,
    )
```

```python
import math

import jax
import jax.numpy as jnp
from jax import lax
from jax.experimental import pallas as pl
from jax.experimental.pallas import tpu as pltpu
from jax.sharding import PartitionSpec as P

LANES = 128


def angle_table(row_count, col_count, modulus):
    row_ids = lax.broadcasted_iota(jnp.int32, (row_count, col_count), 0)
    col_ids = lax.broadcasted_iota(jnp.int32, (row_count, col_count), 1)
    product_mod = row_ids * col_ids % modulus
    angles = product_mod.astype(jnp.float32) * (2.0 * math.pi / modulus)
    return (jnp.cos(angles), jnp.sin(angles))


def split_bf16(value):
    high = value.astype(jnp.bfloat16)
    low = (value - high.astype(jnp.float32)).astype(jnp.bfloat16)
    return high, low


def split_table(value):
    high = lax.reduce_precision(value, exponent_bits=8, mantissa_bits=7)
    return high.astype(jnp.bfloat16), (value - high).astype(jnp.bfloat16)


def mat(a, b):
    return jnp.dot(a, b, preferred_element_type=jnp.float32)


def dot_left(t_hi, t_lo, value):
    v_hi, v_lo = split_bf16(value)
    return mat(t_hi, v_hi) + mat(t_hi, v_lo) + mat(t_lo, v_hi)


def dot_right(value, t_hi, t_lo):
    v_hi, v_lo = split_bf16(value)
    return mat(v_hi, t_hi) + mat(v_lo, t_hi) + mat(v_hi, t_lo)


def spectrum_tables(length):
    half = length // LANES
    blocks = 2 * half
    total = blocks * LANES
    cos_one, sin_one = angle_table(blocks, half, blocks)
    cos_tw, sin_tw = angle_table(blocks, LANES, total)
    cos_two, sin_two = angle_table(LANES, LANES, LANES)
    first = jnp.concatenate([cos_one, -sin_one], axis=0)
    forward = jnp.concatenate(
        [jnp.concatenate([cos_two, -sin_two], 1), jnp.concatenate([sin_two, cos_two], 1)], 0
    )
    backward = jnp.concatenate(
        [jnp.concatenate([cos_two, sin_two], 1), jnp.concatenate([-sin_two, cos_two], 1)], 0
    )
    last = jnp.concatenate([cos_one.T, -sin_one.T], axis=1) / total
    return (
        *split_table(first),
        cos_tw,
        sin_tw,
        *split_table(forward),
        *split_table(backward),
        *split_table(last),
    )


def chain_kernel(
    sub, taps_ref, x_ref, h_ref, og_ref, a1h, a1l, tcr, tsr, w2h, w2l, wbh, wbl, a3h, a3l,
    in_ref, fg_ref, tp_ref, q_s, k_s, v_s, conv_s, hs_s, ws_s, ds_s,
):
    layers, rows, lanes = x_ref.shape
    half = rows // sub
    blocks = 2 * half
    row_id = lax.broadcasted_iota(jnp.int32, (rows, lanes), 0)
    lane_id = lax.broadcasted_iota(jnp.int32, (rows, lanes), 1)
    first_row = row_id == 0
    last_row = row_id == half - 1
    for c in range(1, sub):
        first_row = first_row | (row_id == c * half)
        last_row = last_row | (row_id == c * half + half - 1)

    def fft(signal):
        twc = tcr[...]
        tws = tsr[...]
        parts = []
        for c in range(sub):
            y = dot_left(a1h[...], a1l[...], signal[c * half:(c + 1) * half, :])
            yr, yi = y[:blocks], y[blocks:]
            parts.append(jnp.concatenate([yr * twc + yi * tws, yi * twc - yr * tws], axis=1))
        return dot_right(jnp.concatenate(parts, axis=0), w2h[...], w2l[...])

    def ifft(spec):
        twc = tcr[...]
        tws = tsr[...]
        p = dot_right(spec, wbh[...], wbl[...])
        outs = []
        for c in range(sub):
            pr = p[c * blocks:(c + 1) * blocks, :lanes]
            pi = p[c * blocks:(c + 1) * blocks, lanes:]
            q = jnp.concatenate([pr * twc - pi * tws, pr * tws + pi * twc], axis=0)
            outs.append(dot_left(a3h[...], a3l[...], q))
        return jnp.concatenate(outs, axis=0)

    def back(value, j):
        if j == 0:
            return value
        r1 = pltpu.roll(value, j, 1)
        r2 = pltpu.roll(r1, 1, 0)
        out = jnp.where(lane_id >= j, r1, r2)
        return jnp.where(first_row & (lane_id < j), 0.0, out)

    def ahead(value, j):
        if j == 0:
            return value
        r1 = pltpu.roll(value, lanes - j, 1)
        r2 = pltpu.roll(r1, rows - 1, 0)
        out = jnp.where(lane_id < lanes - j, r1, r2)
        return jnp.where(last_row & (lane_id >= lanes - j), 0.0, out)

    def tap(layer, i, j):
        base = ((layer * 3 + i) * 7 + j) * sub
        w = jnp.full((rows, lanes), taps_ref[base + sub - 1], jnp.float32)
        for c in range(sub - 2, -1, -1):
            w = jnp.where(row_id < (c + 1) * half, taps_ref[base + c], w)
        return w

    def real_imag(spec):
        return spec[:, :lanes], spec[:, lanes:]

    def phase_one(layer, carry):
        x = x_ref[layer].astype(jnp.float32)
        feats = [jnp.zeros((rows, lanes), jnp.float32) for _ in range(3)]
        for j in range(7):
            xs = back(x, j)
            for i in range(3):
                feats[i] = feats[i] + tap(layer, i, j) * xs
        q, k, v = [f.astype(jnp.bfloat16).astype(jnp.float32) for f in feats]
        q_s[layer] = q
        k_s[layer] = k
        v_s[layer] = v
        hspec = fft(h_ref[layer].astype(jnp.float32))
        wspec = fft(k * v)
        hs_s[layer] = hspec
        ws_s[layer] = wspec
        hr, hi = real_imag(hspec)
        wr, wi = real_imag(wspec)
        conv_s[layer] = ifft(jnp.concatenate([hr * wr - hi * wi, hr * wi + hi * wr], axis=1))
        return carry

    lax.fori_loop(0, layers, phase_one, 0, unroll=2)

    def phase_two(step, carried):
        layer = layers - 1 - step
        grad_z = carried * q_s[layer]
        grad_q = carried * conv_s[layer]
        dspec = fft(grad_z)
        ds_s[layer] = dspec
        hr, hi = real_imag(hs_s[layer])
        dr, di = real_imag(dspec)
        grad_w = ifft(jnp.concatenate([hr * dr + hi * di, hr * di - hi * dr], axis=1))
        grads = (grad_q, grad_w * v_s[layer], grad_w * k_s[layer])
        summed = jnp.zeros((rows, lanes), jnp.float32)
        for j in range(7):
            term = tap(layer, 0, j) * grads[0]
            term = term + tap(layer, 1, j) * grads[1]
            term = term + tap(layer, 2, j) * grads[2]
            summed = summed + ahead(term, j)
        rounded = summed.astype(jnp.bfloat16)
        in_ref[layer] = rounded
        x = x_ref[layer].astype(jnp.float32)
        for j in range(7):
            xs = back(x, j)
            for i in range(3):
                prod = grads[i] * xs
                for c in range(sub):
                    row = (i * 7 + j) * sub + c
                    part = prod[c * half:c * half + 8, :]
                    for r in range(c * half + 8, (c + 1) * half, 8):
                        part = part + prod[r:r + 8, :]
                    tp_ref[layer, row] = part
        return rounded.astype(jnp.float32)

    lax.fori_loop(0, layers, phase_two, og_ref[...].astype(jnp.float32))

    def phase_three(layer, carry):
        wr, wi = real_imag(ws_s[layer])
        dr, di = real_imag(ds_s[layer])
        fg_ref[layer] = ifft(jnp.concatenate([wr * dr + wi * di, wr * di - wi * dr], axis=1))
        return carry

    lax.fori_loop(0, layers, phase_three, 0, unroll=2)


def run_chain(x_all, h_all, og, taps_all):
    layers, rows, _ = x_all.shape
    sub = taps_all.shape[3]
    half = rows // sub
    length = half * LANES
    blocks = 2 * half
    tables = spectrum_tables(length)
    vmem = pl.BlockSpec(memory_space=pltpu.VMEM)
    spec_shape = pltpu.VMEM((layers, sub * blocks, 2 * LANES), jnp.float32)
    sig_shape = pltpu.VMEM((layers, rows, LANES), jnp.float32)
    in_k, fg_k, tp_k = pl.pallas_call(
        lambda *refs: chain_kernel(sub, *refs),
        out_shape=(
            jax.ShapeDtypeStruct((layers, rows, LANES), jnp.bfloat16),
            jax.ShapeDtypeStruct((layers, rows, LANES), jnp.float32),
            jax.ShapeDtypeStruct((layers, 21 * sub, 8, LANES), jnp.float32),
        ),
        in_specs=[pl.BlockSpec(memory_space=pltpu.SMEM)] + [vmem] * 13,
        out_specs=(vmem, vmem, vmem),
        scratch_shapes=[sig_shape] * 4 + [spec_shape] * 3,
        compiler_params=pltpu.CompilerParams(vmem_limit_bytes=48 * 1024 * 1024),
        name="hyena_chain",
    )(
        taps_all.reshape(-1),
        x_all,
        h_all,
        og.reshape(rows, LANES),
        *tables,
    )
    tap_grad = jnp.sum(tp_k, axis=(2, 3)).reshape(layers, 3, 7, sub)
    return in_k.reshape(layers, sub, length), fg_k.reshape(layers, sub, length), tap_grad


def exact_pieces(value):
    pieces = []
    rest = value
    for _ in range(3):
        high = lax.reduce_precision(rest, exponent_bits=8, mantissa_bits=7)
        pieces.append(high.astype(jnp.bfloat16))
        rest = rest - high
    return jnp.concatenate(pieces, axis=-1)


def joined(pieces):
    third = pieces.shape[-1] // 3
    parts = [pieces[..., i * third:(i + 1) * third].astype(jnp.float32) for i in range(3)]
    return parts[0] + parts[1] + parts[2]


def shards(inputs, out_grad, filters, conv_taps):
    sec_n = lax.axis_size("section")
    ctx_n = lax.axis_size("ctx")
    sec = lax.axis_index("section")
    ctx = lax.axis_index("ctx")
    channels = filters.shape[1]
    length = filters.shape[2]
    sub = channels // sec_n
    tok_dev = inputs.shape[2]
    span = sub * length
    og = lax.dynamic_index_in_dim(
        out_grad.reshape(ctx_n, sec_n, sub, tok_dev), sec, 1, keepdims=False
    )
    sent = jnp.concatenate([inputs[0].reshape(ctx_n, channels, tok_dev), og], axis=1)
    got = lax.all_to_all(sent, "ctx", split_axis=0, concat_axis=2, tiled=True)[0]
    x_ctx = got[:channels]
    og = got[channels:]
    rows = sub * length // LANES
    taps_c = lax.dynamic_slice_in_dim(conv_taps[0], ctx * channels, channels, 2)
    taps_c = jnp.moveaxis(taps_c.reshape(3, 7, sec_n, sub), 2, 0).reshape(sec_n, 21 * sub)
    taps_c = exact_pieces(taps_c)
    taps_c = jnp.pad(taps_c, ((0, 0), (0, LANES - taps_c.shape[1])))
    sent = jnp.concatenate(
        [
            x_ctx.reshape(sec_n, rows, LANES),
            filters[0].reshape(sec_n, rows, LANES),
            taps_c[:, None, :],
        ],
        axis=1,
    )
    got = lax.all_to_all(sent, "section", split_axis=0, concat_axis=0, tiled=True)
    x_all = got[:, :rows]
    h_all = got[:, rows:2 * rows]
    taps_all = joined(got[:, 2 * rows, :63 * sub]).reshape(sec_n, 3, 7, sub)
    in_all, filter_grad, tap_grad = run_chain(x_all, h_all, og, taps_all)
    fg_high, fg_low = split_table(filter_grad.reshape(sec_n, span))
    taps_out = exact_pieces(tap_grad.reshape(sec_n, 21 * sub))
    taps_out = jnp.pad(taps_out, ((0, 0), (0, LANES - taps_out.shape[1])))
    sent = jnp.concatenate(
        [fg_high, fg_low, in_all.reshape(sec_n, span), taps_out],
        axis=1,
    )
    got3 = lax.all_to_all(
        sent.reshape(sec_n, -1, LANES), "section", split_axis=0, concat_axis=0, tiled=True
    )
    got = got3.reshape(sec_n, -1)
    fg = got[:, :span].astype(jnp.float32) + got[:, span:2 * span].astype(jnp.float32)
    fg = fg.reshape(1, channels, length)
    ig = got3[:, 2 * rows:3 * rows].reshape(sec_n, sub, ctx_n, tok_dev)
    ig = jnp.transpose(ig, (2, 0, 1, 3)).reshape(ctx_n, channels, tok_dev)
    tg = jnp.moveaxis(joined(got[:, 3 * span:3 * span + 63 * sub]).reshape(sec_n, 3, 7, sub), 0, 2)
    tg = tg.reshape(1, 3, 7, channels)
    ig = lax.all_to_all(ig, "ctx", split_axis=0, concat_axis=0, tiled=True)
    return (ig.reshape(1, ctx_n * channels, tok_dev), fg, tg)


def solution(mesh):
    placed = (
        P("section", None, "ctx"),
        P(None, "ctx"),
        P("section", "ctx", None),
        P("section", None, None, None),
    )
    return jax.shard_map(
        shards,
        mesh=mesh,
        in_specs=placed,
        out_specs=(
            P("section", None, "ctx"),
            P("section", "ctx", None),
            P("section", None, None, "ctx"),
        ),
        check_vma=False,
    )
```

```python
import math

import jax
import jax.numpy as jnp
from jax import lax
from jax.experimental import pallas as pl
from jax.experimental.pallas import tpu as pltpu
from jax.sharding import PartitionSpec as P

LANES = 128


def angle_table(row_count, col_count, modulus):
    row_ids = lax.broadcasted_iota(jnp.int32, (row_count, col_count), 0)
    col_ids = lax.broadcasted_iota(jnp.int32, (row_count, col_count), 1)
    product_mod = row_ids * col_ids % modulus
    angles = product_mod.astype(jnp.float32) * (2.0 * math.pi / modulus)
    return (jnp.cos(angles), jnp.sin(angles))


def split_bf16(value):
    high = value.astype(jnp.bfloat16)
    low = (value - high.astype(jnp.float32)).astype(jnp.bfloat16)
    return high, low


def split_table(value):
    high = lax.reduce_precision(value, exponent_bits=8, mantissa_bits=7)
    return high.astype(jnp.bfloat16), (value - high).astype(jnp.bfloat16)


def mat(a, b):
    return jnp.dot(a, b, preferred_element_type=jnp.float32)


def dot_left(t_hi, t_lo, value):
    v_hi, v_lo = split_bf16(value)
    return mat(t_hi, v_hi) + mat(t_hi, v_lo) + mat(t_lo, v_hi)


def dot_right(value, t_hi, t_lo):
    v_hi, v_lo = split_bf16(value)
    return mat(v_hi, t_hi) + mat(v_lo, t_hi) + mat(v_hi, t_lo)


def spectrum_tables(length):
    half = length // LANES
    blocks = 2 * half
    total = blocks * LANES
    cos_one, sin_one = angle_table(blocks, half, blocks)
    cos_tw, sin_tw = angle_table(blocks, LANES, total)
    cos_two, sin_two = angle_table(LANES, LANES, LANES)
    first = jnp.concatenate([cos_one, -sin_one], axis=0)
    forward = jnp.concatenate(
        [jnp.concatenate([cos_two, -sin_two], 1), jnp.concatenate([sin_two, cos_two], 1)], 0
    )
    backward = jnp.concatenate(
        [jnp.concatenate([cos_two, sin_two], 1), jnp.concatenate([-sin_two, cos_two], 1)], 0
    )
    last = jnp.concatenate([cos_one.T, -sin_one.T], axis=1) / total
    return (
        *split_table(first),
        cos_tw,
        sin_tw,
        *split_table(forward),
        *split_table(backward),
        *split_table(last),
    )


def chain_kernel(
    sub, taps_ref, x_ref, h_ref, og_ref, a1h, a1l, tcr, tsr, w2h, w2l, wbh, wbl, a3h, a3l,
    in_ref, fg_ref, tp_ref, q_s, k_s, v_s, conv_s, hs_s, ws_s, ds_s,
):
    layers, rows, lanes = x_ref.shape
    half = rows // sub
    blocks = 2 * half
    row_id = lax.broadcasted_iota(jnp.int32, (rows, lanes), 0)
    lane_id = lax.broadcasted_iota(jnp.int32, (rows, lanes), 1)
    first_row = row_id == 0
    last_row = row_id == half - 1
    for c in range(1, sub):
        first_row = first_row | (row_id == c * half)
        last_row = last_row | (row_id == c * half + half - 1)

    def fft(signal):
        twc = tcr[...]
        tws = tsr[...]
        parts = []
        for c in range(sub):
            y = dot_left(a1h[...], a1l[...], signal[c * half:(c + 1) * half, :])
            yr, yi = y[:blocks], y[blocks:]
            parts.append(jnp.concatenate([yr * twc + yi * tws, yi * twc - yr * tws], axis=1))
        return dot_right(jnp.concatenate(parts, axis=0), w2h[...], w2l[...])

    def ifft(spec):
        twc = tcr[...]
        tws = tsr[...]
        p = dot_right(spec, wbh[...], wbl[...])
        outs = []
        for c in range(sub):
            pr = p[c * blocks:(c + 1) * blocks, :lanes]
            pi = p[c * blocks:(c + 1) * blocks, lanes:]
            q = jnp.concatenate([pr * twc - pi * tws, pr * tws + pi * twc], axis=0)
            outs.append(dot_left(a3h[...], a3l[...], q))
        return jnp.concatenate(outs, axis=0)

    def back(value, j):
        if j == 0:
            return value
        r1 = pltpu.roll(value, j, 1)
        r2 = pltpu.roll(r1, 1, 0)
        out = jnp.where(lane_id >= j, r1, r2)
        return jnp.where(first_row & (lane_id < j), 0.0, out)

    def ahead(value, j):
        if j == 0:
            return value
        r1 = pltpu.roll(value, lanes - j, 1)
        r2 = pltpu.roll(r1, rows - 1, 0)
        out = jnp.where(lane_id < lanes - j, r1, r2)
        return jnp.where(last_row & (lane_id >= lanes - j), 0.0, out)

    def tap(layer, i, j):
        base = ((layer * 3 + i) * 7 + j) * sub
        w = jnp.full((rows, lanes), taps_ref[base + sub - 1], jnp.float32)
        for c in range(sub - 2, -1, -1):
            w = jnp.where(row_id < (c + 1) * half, taps_ref[base + c], w)
        return w

    def real_imag(spec):
        return spec[:, :lanes], spec[:, lanes:]

    def phase_one(layer, carry):
        x = x_ref[layer].astype(jnp.float32)
        feats = [jnp.zeros((rows, lanes), jnp.float32) for _ in range(3)]
        for j in range(7):
            xs = back(x, j)
            for i in range(3):
                feats[i] = feats[i] + tap(layer, i, j) * xs
        q, k, v = [f.astype(jnp.bfloat16).astype(jnp.float32) for f in feats]
        q_s[layer] = q
        k_s[layer] = k
        v_s[layer] = v
        hspec = fft(h_ref[layer].astype(jnp.float32))
        wspec = fft(k * v)
        hs_s[layer] = hspec
        ws_s[layer] = wspec
        hr, hi = real_imag(hspec)
        wr, wi = real_imag(wspec)
        conv_s[layer] = ifft(jnp.concatenate([hr * wr - hi * wi, hr * wi + hi * wr], axis=1))
        return carry

    lax.fori_loop(0, layers, phase_one, 0, unroll=4)

    def phase_two(step, carried):
        layer = layers - 1 - step
        grad_z = carried * q_s[layer]
        grad_q = carried * conv_s[layer]
        dspec = fft(grad_z)
        ds_s[layer] = dspec
        hr, hi = real_imag(hs_s[layer])
        dr, di = real_imag(dspec)
        grad_w = ifft(jnp.concatenate([hr * dr + hi * di, hr * di - hi * dr], axis=1))
        grads = (grad_q, grad_w * v_s[layer], grad_w * k_s[layer])
        summed = jnp.zeros((rows, lanes), jnp.float32)
        for j in range(7):
            term = tap(layer, 0, j) * grads[0]
            term = term + tap(layer, 1, j) * grads[1]
            term = term + tap(layer, 2, j) * grads[2]
            summed = summed + ahead(term, j)
        rounded = summed.astype(jnp.bfloat16)
        in_ref[layer] = rounded
        x = x_ref[layer].astype(jnp.float32)
        for j in range(7):
            xs = back(x, j)
            for i in range(3):
                prod = grads[i] * xs
                for c in range(sub):
                    row = (i * 7 + j) * sub + c
                    part = prod[c * half:c * half + 8, :]
                    for r in range(c * half + 8, (c + 1) * half, 8):
                        part = part + prod[r:r + 8, :]
                    tp_ref[layer, row] = part
        return rounded.astype(jnp.float32)

    lax.fori_loop(0, layers, phase_two, og_ref[...].astype(jnp.float32), unroll=2)

    def phase_three(layer, carry):
        wr, wi = real_imag(ws_s[layer])
        dr, di = real_imag(ds_s[layer])
        fg_ref[layer] = ifft(jnp.concatenate([wr * dr + wi * di, wr * di - wi * dr], axis=1))
        return carry

    lax.fori_loop(0, layers, phase_three, 0, unroll=4)


def run_chain(x_all, h_all, og, taps_all):
    layers, rows, _ = x_all.shape
    sub = taps_all.shape[3]
    half = rows // sub
    length = half * LANES
    blocks = 2 * half
    tables = spectrum_tables(length)
    vmem = pl.BlockSpec(memory_space=pltpu.VMEM)
    spec_shape = pltpu.VMEM((layers, sub * blocks, 2 * LANES), jnp.float32)
    sig_shape = pltpu.VMEM((layers, rows, LANES), jnp.float32)
    in_k, fg_k, tp_k = pl.pallas_call(
        lambda *refs: chain_kernel(sub, *refs),
        out_shape=(
            jax.ShapeDtypeStruct((layers, rows, LANES), jnp.bfloat16),
            jax.ShapeDtypeStruct((layers, rows, LANES), jnp.float32),
            jax.ShapeDtypeStruct((layers, 21 * sub, 8, LANES), jnp.float32),
        ),
        in_specs=[pl.BlockSpec(memory_space=pltpu.SMEM)] + [vmem] * 13,
        out_specs=(vmem, vmem, vmem),
        scratch_shapes=[sig_shape] * 4 + [spec_shape] * 3,
        compiler_params=pltpu.CompilerParams(vmem_limit_bytes=48 * 1024 * 1024),
        name="hyena_chain",
    )(
        taps_all.reshape(-1),
        x_all,
        h_all,
        og.reshape(rows, LANES),
        *tables,
    )
    tap_grad = jnp.sum(tp_k, axis=(2, 3)).reshape(layers, 3, 7, sub)
    return in_k.reshape(layers, sub, length), fg_k.reshape(layers, sub, length), tap_grad


def exact_pieces(value):
    pieces = []
    rest = value
    for _ in range(3):
        high = lax.reduce_precision(rest, exponent_bits=8, mantissa_bits=7)
        pieces.append(high.astype(jnp.bfloat16))
        rest = rest - high
    return jnp.concatenate(pieces, axis=-1)


def joined(pieces):
    third = pieces.shape[-1] // 3
    parts = [pieces[..., i * third:(i + 1) * third].astype(jnp.float32) for i in range(3)]
    return parts[0] + parts[1] + parts[2]


def shards(inputs, out_grad, filters, conv_taps):
    sec_n = lax.axis_size("section")
    ctx_n = lax.axis_size("ctx")
    sec = lax.axis_index("section")
    ctx = lax.axis_index("ctx")
    channels = filters.shape[1]
    length = filters.shape[2]
    sub = channels // sec_n
    tok_dev = inputs.shape[2]
    span = sub * length
    og = lax.dynamic_index_in_dim(
        out_grad.reshape(ctx_n, sec_n, sub, tok_dev), sec, 1, keepdims=False
    )
    sent = jnp.concatenate([inputs[0].reshape(ctx_n, channels, tok_dev), og], axis=1)
    got = lax.all_to_all(sent, "ctx", split_axis=0, concat_axis=2, tiled=True)[0]
    x_ctx = got[:channels]
    og = got[channels:]
    rows = sub * length // LANES
    taps_c = lax.dynamic_slice_in_dim(conv_taps[0], ctx * channels, channels, 2)
    taps_c = jnp.moveaxis(taps_c.reshape(3, 7, sec_n, sub), 2, 0).reshape(sec_n, 21 * sub)
    taps_c = exact_pieces(taps_c)
    taps_c = jnp.pad(taps_c, ((0, 0), (0, LANES - taps_c.shape[1])))
    sent = jnp.concatenate(
        [
            x_ctx.reshape(sec_n, rows, LANES),
            filters[0].reshape(sec_n, rows, LANES),
            taps_c[:, None, :],
        ],
        axis=1,
    )
    got = lax.all_to_all(sent, "section", split_axis=0, concat_axis=0, tiled=True)
    x_all = got[:, :rows]
    h_all = got[:, rows:2 * rows]
    taps_all = joined(got[:, 2 * rows, :63 * sub]).reshape(sec_n, 3, 7, sub)
    in_all, filter_grad, tap_grad = run_chain(x_all, h_all, og, taps_all)
    fg_high, fg_low = split_table(filter_grad.reshape(sec_n, span))
    taps_out = exact_pieces(tap_grad.reshape(sec_n, 21 * sub))
    taps_out = jnp.pad(taps_out, ((0, 0), (0, LANES - taps_out.shape[1])))
    sent = jnp.concatenate(
        [fg_high, fg_low, in_all.reshape(sec_n, span), taps_out],
        axis=1,
    )
    got3 = lax.all_to_all(
        sent.reshape(sec_n, -1, LANES), "section", split_axis=0, concat_axis=0, tiled=True
    )
    got = got3.reshape(sec_n, -1)
    fg = got[:, :span].astype(jnp.float32) + got[:, span:2 * span].astype(jnp.float32)
    fg = fg.reshape(1, channels, length)
    ig = got3[:, 2 * rows:3 * rows].reshape(sec_n, sub, ctx_n, tok_dev)
    ig = jnp.transpose(ig, (2, 0, 1, 3)).reshape(ctx_n, channels, tok_dev)
    tg = jnp.moveaxis(joined(got[:, 3 * span:3 * span + 63 * sub]).reshape(sec_n, 3, 7, sub), 0, 2)
    tg = tg.reshape(1, 3, 7, channels)
    ig = lax.all_to_all(ig, "ctx", split_axis=0, concat_axis=0, tiled=True)
    return (ig.reshape(1, ctx_n * channels, tok_dev), fg, tg)


def solution(mesh):
    placed = (
        P("section", None, "ctx"),
        P(None, "ctx"),
        P("section", "ctx", None),
        P("section", None, None, None),
    )
    return jax.shard_map(
        shards,
        mesh=mesh,
        in_specs=placed,
        out_specs=(
            P("section", None, "ctx"),
            P("section", "ctx", None),
            P("section", None, None, "ctx"),
        ),
        check_vma=False,
    )
```
